256 devices in a mesh: seq: 32 (over z_lo, y, core), head: 8 (over x, z_hi).
Axes of the slice: x: 4, y: 4, z: 8 (z_hi: 2, z_lo: 4; z = z_hi * 4 + z_lo), core: 2. Of those that a mesh axis runs over, the one named last changes fastest.
Arguments:
- queries: bfloat16 [16384, 1024], P('seq', 'head'), may hold values from -2.5 to 2.5
- keys: bfloat16 [16384, 1024], P('seq', 'head'), may hold values from -2.5 to 2.5
- values: bfloat16 [16384, 1024], P('seq', 'head'), may hold values from -6 to 6
- attn_out: bfloat16 [16384, 1024], P('seq', 'head'), may hold values from -6 to 6
- out_grad: bfloat16 [16384, 1024], P('seq', 'head'), may hold values from -6 to 6
- lse: float32 [8, 16384], P('head', 'seq'), may hold values from 3.5 to 5.5
- trace_id: int32 [16384], replicated, may hold values from 0 to 127, never falling along the last dimension, each value on 1 to 384 neighbouring positions
- key_tiles: int32 [128, 48], P('seq'), may hold values from 0 to 127, as said below
- tile_count: int32 [128], P('seq'), may hold values from 1 to 48, as said below
- w_query: bfloat16 [1024, 1024], P(None, 'head'), may hold values from -0.1875 to 0.1875
- w_key: bfloat16 [1024, 1024], P(None, 'head'), may hold values from -0.1875 to 0.1875
- w_value: bfloat16 [1024, 1024], P(None, 'head'), may hold values from -0.1875 to 0.1875
- w_out: bfloat16 [1024, 1024], P('head'), may hold values from -0.1875 to 0.1875
Outputs:
- d_input: bfloat16 [16384, 1024], P('seq', 'head')
The draws below stay inside these ranges and needn't reach their ends.
Inputs may be any that keep to these rules, and one draw needn't show every extreme that they name: `key_tiles`: each row lists 48 different key tiles and never its own tile; entries from position tile_count onward are not used. `tile_count`: some query tile uses all 48 entries. `trace_id`: trace numbers never fall along the tokens; one trace spans 384 tokens, none more.
All inputs are finite; a program needn't handle non-finite values.
Results may differ from the reference program's by a relative error of at most 0.015.
Values may be sent and summed in bfloat16 or wider, within the bound.
No kernel may reach another device: no remote copies, remote signals or barrier semaphores. Data moves between devices by JAX's collectives and lax.ppermute only.
A program may use at most 64 MiB of HBM per device.

```python
import math
import jax
import jax.numpy as jnp
import numpy as np
from jax import lax

HEADS = 8
HD = 128
D = 1024
TILE = 128
SEL = 48
TOK_DEV = 512
TOKENS = 16384
NT = 128
TILES_DEV = 4
N_SEQ = 32


def draw_key_tiles(key, part):
    ranks = jax.random.randint(key, (NT, NT), 0, 2 ** 20)
    ranks = ranks * NT + jnp.arange(NT)[None, :]
    own_tile = jnp.arange(NT)[:, None] == jnp.arange(NT)[None, :]
    ranks = jnp.where(own_tile, jnp.int32(2 ** 30), ranks)
    order = jnp.argsort(ranks, axis=1)
    return order[:, :SEL].astype(jnp.int32)


def draw_tile_count(key, part):
    first, second, third = jax.random.split(key, 3)
    level = jax.random.randint(first, (NT // TILES_DEV,), 0, 4)
    factor = jnp.power(2, level)
    upper = jnp.repeat(SEL * factor // 8, TILES_DEV)
    counts = jax.random.randint(second, (NT,), 1, upper + 1)
    chosen = jax.random.randint(third, (), 0, NT)
    counts = jnp.where(jnp.arange(NT) == chosen, SEL, counts)
    return counts.astype(jnp.int32)


def level_of(key, extent, cuts, low, high):
    gain = 1.0
    for position, parts in cuts:
        draws = jax.random.uniform(jax.random.fold_in(jax.random.fold_in(key, 6), position), (parts,), jnp.float32, low / len(cuts), high / len(cuts))
        gain = gain * jnp.repeat(jnp.exp(draws), extent[position] // parts).reshape((-1,) + (1,) * (len(extent) - 1 - position))
    return gain


def profile(count, total, most, lean):
    portions = [(1 << 20) // math.isqrt(grade ** lean) + 1 for grade in range(2, count + 1)]
    rest, given = total - most - (count - 1), [1] * (count - 1)
    while rest > 0:
        candidates = [i for i in range(count - 1) if given[i] < most]
        pool, budget = sum([portions[i] for i in candidates]), rest
        for i in candidates:
            addition = min(most - given[i], max(1, budget * portions[i] // pool), rest)
            given[i] = given[i] + addition
            rest = rest - addition
    return np.array([most] + given)


def uneven_parts(stream_key, count, total, bound, slope):
    if count == 2:
        one = jax.random.randint(stream_key, (), max(1, total - bound), min(bound, total - 1) + 1)
        return jnp.stack([one, total - one])
    tallies = jnp.asarray(profile(count, total, bound, slope), jnp.int32)
    twos = (count - 1) // 2
    source_of, taker = tallies[1:1 + 2 * twos:2], tallies[2:2 + 2 * twos:2]
    room = jnp.minimum(source_of - 1, bound - taker)
    passed = jax.random.randint(jax.random.fold_in(stream_key, 1), (twos,), 0, 1 << 20) % (room + 1)
    tallies = tallies.at[1:1 + 2 * twos:2].set(source_of - passed).at[2:2 + 2 * twos:2].set(taker + passed)
    return tallies[jax.random.permutation(jax.random.fold_in(stream_key, 2), count)]


def scatter_about(rng, dims, width, bound, shards=(), dtype=jnp.bfloat16):
    loudness = level_of(rng, dims, shards, -0.22, 0.18) if shards else 1.0
    values = jax.random.normal(rng, dims, jnp.float32) * width * loudness
    return jnp.minimum(jnp.maximum(values, -bound), bound).astype(dtype)


def setup_inputs(seed: int = 0) -> dict:
    splits = jax.random.split(jax.random.key(seed), 14)
    queries = scatter_about(splits[0], (TOKENS, D), 1.0, 2.5, ((0, 32), (1, 8)))
    keys = scatter_about(splits[1], (TOKENS, D), 1.0, 2.5, ((0, 32), (1, 8)))
    values = scatter_about(splits[2], (TOKENS, D), 1.0, 6.0, ((0, 32), (1, 8)))
    attn_out = scatter_about(splits[3], (TOKENS, D), 1.0, 6.0, ((0, 32), (1, 8)))
    out_grad = scatter_about(splits[4], (TOKENS, D), 1.0, 6.0, ((0, 32), (1, 8)))
    lse = jnp.clip(3.5 + 2.0 * jax.random.uniform(splits[5], (HEADS, TOKENS), jnp.float32) ** level_of(splits[5], (HEADS, TOKENS), ((0, 8), (1, 32)), -0.2, 0.2), 3.5, 5.5)
    trace_id = jnp.searchsorted(jnp.cumsum(uneven_parts(splits[6], TOKENS // TILE, TOKENS, 3 * TILE, 2)), jnp.arange(TOKENS), side="right").astype(jnp.int32)
    key_tiles = draw_key_tiles(jax.random.fold_in(splits[13], 71), 0)
    tile_count = draw_tile_count(jax.random.fold_in(splits[13], 71), 0)
    w_query = scatter_about(splits[9], (D, D), D ** -0.5, 0.1875, ((1, 8),))
    w_key = scatter_about(splits[10], (D, D), D ** -0.5, 0.1875, ((1, 8),))
    w_value = scatter_about(splits[11], (D, D), D ** -0.5, 0.1875, ((1, 8),))
    w_out = scatter_about(splits[12], (D, D), D ** -0.5, 0.1875, ((0, 8),))
    return {"queries": queries, "keys": keys, "values": values, "attn_out": attn_out, "out_grad": out_grad, "lse": lse, "trace_id": trace_id, "key_tiles": key_tiles, "tile_count": tile_count, "w_query": w_query, "w_key": w_key, "w_value": w_value, "w_out": w_out}


def head_grads(query_part, key_part, value_part, grad_part, norm_part, delta_part, admit):
    scale = HD ** -0.5
    scores = jnp.dot(query_part, key_part.T, preferred_element_type=jnp.float32) * scale
    probs = jnp.where(admit, jnp.exp(scores - norm_part[:, None]), 0.0)
    value_grad = jnp.dot(probs.astype(jnp.bfloat16).T, grad_part, preferred_element_type=jnp.float32)
    prob_grad = jnp.dot(grad_part, value_part.T, preferred_element_type=jnp.float32)
    score_grad = (probs * (prob_grad - delta_part[:, None]) * scale).astype(jnp.bfloat16)
    query_grad = jnp.dot(score_grad, key_part, preferred_element_type=jnp.float32)
    key_grad = jnp.dot(score_grad.T, query_part, preferred_element_type=jnp.float32)
    return query_grad, key_grad, value_grad


def settle(total):
    part = lax.optimization_barrier(total.astype(jnp.bfloat16))
    return part.astype(jnp.float32)


def reference(queries, keys, values, attn_out, out_grad, lse, trace_id, key_tiles, tile_count, w_query, w_key, w_value, w_out):
    d_attn = jnp.dot(out_grad, w_out.T, preferred_element_type=jnp.float32).astype(jnp.bfloat16)
    product = d_attn.astype(jnp.float32) * attn_out.astype(jnp.float32)
    delta = jnp.sum(product.reshape(TOKENS, HEADS, HD), axis=2).T
    slots = jnp.arange(SEL)[None, :] < tile_count[:, None]
    allowed = jnp.any((key_tiles[:, :, None] == jnp.arange(NT)[None, None, :]) & slots[:, :, None], axis=1)

    def per_block(carry, block):
        key_sum, value_sum = carry
        start = (block * TOK_DEV).astype(jnp.int32)
        rows = lax.dynamic_slice_in_dim(allowed, (block * TILES_DEV).astype(jnp.int32), TILES_DEV, 0)
        trace_rows = lax.dynamic_slice_in_dim(trace_id, start, TOK_DEV, 0)
        admit = jnp.repeat(jnp.repeat(rows, TILE, axis=0), TILE, axis=1) & (trace_rows[:, None] != trace_id[None, :])
        query_rows = lax.dynamic_slice_in_dim(queries, start, TOK_DEV, 0)
        grad_rows = lax.dynamic_slice_in_dim(d_attn, start, TOK_DEV, 0)
        norm_rows = lax.dynamic_slice_in_dim(lse, start, TOK_DEV, 1)
        delta_rows = lax.dynamic_slice_in_dim(delta, start, TOK_DEV, 1)

        def per_head(head):
            offset = (head * HD).astype(jnp.int32)
            return head_grads(
                lax.dynamic_slice_in_dim(query_rows, offset, HD, 1),
                lax.dynamic_slice_in_dim(keys, offset, HD, 1),
                lax.dynamic_slice_in_dim(values, offset, HD, 1),
                lax.dynamic_slice_in_dim(grad_rows, offset, HD, 1),
                lax.dynamic_index_in_dim(norm_rows, head, 0, keepdims=False),
                lax.dynamic_index_in_dim(delta_rows, head, 0, keepdims=False),
                admit)

        query_grad, key_grad, value_grad = lax.map(per_head, jnp.arange(HEADS).astype(jnp.int32))
        query_block = jnp.transpose(query_grad, (1, 0, 2)).reshape(TOK_DEV, D)
        key_block = jnp.transpose(key_grad, (1, 0, 2)).reshape(TOKENS, D)
        value_block = jnp.transpose(value_grad, (1, 0, 2)).reshape(TOKENS, D)
        return (key_sum + settle(key_block), value_sum + settle(value_block)), query_block

    zeros = jnp.zeros((TOKENS, D), jnp.float32)
    (key_sum, value_sum), query_blocks = lax.scan(per_block, (zeros, zeros), jnp.arange(N_SEQ).astype(jnp.int32))
    d_query = query_blocks.reshape(TOKENS, D).astype(jnp.bfloat16)
    d_key = key_sum.astype(jnp.bfloat16)
    d_value = value_sum.astype(jnp.bfloat16)
    total = jnp.dot(d_query, w_query.T, preferred_element_type=jnp.float32)
    total = total + jnp.dot(d_key, w_key.T, preferred_element_type=jnp.float32)
    total = total + jnp.dot(d_value, w_value.T, preferred_element_type=jnp.float32)
    return total.astype(jnp.bfloat16)
```

```python
import jax
import jax.numpy as jnp
from jax import lax
from jax.sharding import PartitionSpec as P

HD = 128
TILE = 128
SEL = 48


def from_behind(value, axis, by):
    count = lax.axis_size(axis)
    return lax.ppermute(value, axis, [(i, (i + by) % count) for i in range(count)])


def pair_grads(query_heads, key_heads, value_heads, grad_heads, norm_rows, delta_rows, admit):
    scale = query_heads.shape[-1] ** (-0.5)
    scores = (
        jnp.einsum("rhd,chd->hrc", query_heads, key_heads, preferred_element_type=jnp.float32)
        * scale
    )
    probs = jnp.where(admit[None], jnp.exp(scores - norm_rows[:, :, None]), 0.0)
    value_grad = jnp.einsum(
        "hrc,rhd->chd", probs.astype(jnp.bfloat16), grad_heads, preferred_element_type=jnp.float32
    )
    prob_grad = jnp.einsum(
        "rhd,chd->hrc", grad_heads, value_heads, preferred_element_type=jnp.float32
    )
    score_grad = (probs * (prob_grad - delta_rows[:, :, None]) * scale).astype(jnp.bfloat16)
    query_grad = jnp.einsum(
        "hrc,chd->rhd", score_grad, key_heads, preferred_element_type=jnp.float32
    )
    key_grad = jnp.einsum(
        "hrc,rhd->chd", score_grad, query_heads, preferred_element_type=jnp.float32
    )
    return (query_grad, key_grad, value_grad)


def settle(total):
    part = lax.optimization_barrier(total.astype(jnp.bfloat16))
    return part.astype(jnp.float32)


def per_device(
    queries,
    keys,
    values,
    attn_out,
    out_grad,
    lse,
    trace_id,
    key_tiles,
    tile_count,
    w_query,
    w_key,
    w_value,
    w_out,
):
    tokens_here, width = queries.shape
    heads_here = width // HD
    seq_count = lax.axis_size("seq")
    seq_index = lax.axis_index("seq")
    tiles_here = tokens_here // TILE
    d_attn = lax.dot_general(
        lax.all_gather(out_grad, "head", axis=1, tiled=True),
        w_out,
        (((1,), (1,)), ((), ())),
        preferred_element_type=jnp.float32,
    ).astype(jnp.bfloat16)
    product = d_attn.astype(jnp.float32) * attn_out.astype(jnp.float32)
    delta = jnp.sum(product.reshape(tokens_here, heads_here, HD), axis=2).T
    query_heads = queries.reshape(tokens_here, heads_here, HD)
    key_heads = keys.reshape(tokens_here, heads_here, HD)
    value_heads = values.reshape(tokens_here, heads_here, HD)
    grad_heads = d_attn.reshape(tokens_here, heads_here, HD)
    trace_here = lax.dynamic_slice_in_dim(trace_id, seq_index * tokens_here, tokens_here, 0)
    slots = jnp.arange(SEL)[None, :] < tile_count[:, None]
    tile_range = jnp.arange(seq_count * tiles_here)
    allowed = jnp.any(
        (key_tiles[:, :, None] == tile_range[None, None, :]) & slots[:, :, None], axis=1
    )

    def visit(key_block, value_block, first_tile):
        block_tiles = key_block.shape[0] // TILE
        listed = lax.dynamic_slice(allowed, (0, first_tile), (tiles_here, block_tiles))
        trace_keys = lax.dynamic_slice_in_dim(trace_id, first_tile * TILE, key_block.shape[0], 0)
        admit = jnp.repeat(jnp.repeat(listed, TILE, axis=0), TILE, axis=1) & (
            trace_here[:, None] != trace_keys[None, :]
        )
        return pair_grads(query_heads, key_block, value_block, grad_heads, lse, delta, admit)

    kv_all = lax.all_gather(jnp.stack([key_heads, value_heads]), "seq", axis=1, tiled=True)
    total_tokens = kv_all.shape[1]
    chunk = min(total_tokens, 2048)
    query_sum = None
    key_parts, value_parts = [], []
    for first in range(0, total_tokens, chunk):
        query_add, key_add, value_add = visit(
            kv_all[0, first:first + chunk], kv_all[1, first:first + chunk], first // TILE
        )
        query_sum = query_add if query_sum is None else query_sum + query_add
        key_parts.append(key_add)
        value_parts.append(value_add)
    parts = jnp.stack([jnp.concatenate(key_parts), jnp.concatenate(value_parts)])
    parts = parts.astype(jnp.bfloat16).astype(jnp.float32)
    sums = lax.psum_scatter(parts, "seq", scatter_dimension=1, tiled=True)
    key_sum, value_sum = (sums[0], sums[1])
    d_query = query_sum.astype(jnp.bfloat16).reshape(tokens_here, width)
    d_key = key_sum.astype(jnp.bfloat16).reshape(tokens_here, width)
    d_value = value_sum.astype(jnp.bfloat16).reshape(tokens_here, width)
    contract = (((1,), (1,)), ((), ()))
    total = lax.dot_general(w_query, d_query, contract, preferred_element_type=jnp.float32)
    total = total + lax.dot_general(w_key, d_key, contract, preferred_element_type=jnp.float32)
    d_input = lax.psum_scatter(
        total + lax.dot_general(w_value, d_value, contract, preferred_element_type=jnp.float32),
        "head",
        scatter_dimension=0,
        tiled=True,
    )
    return d_input.T.astype(jnp.bfloat16)


def solution(mesh):
    in_specs = (
        P("seq", "head"),
        P("seq", "head"),
        P("seq", "head"),
        P("seq", "head"),
        P("seq", "head"),
        P("head", "seq"),
        P(),
        P("seq", None),
        P("seq"),
        P(None, "head"),
        P(None, "head"),
        P(None, "head"),
        P("head", None),
    )
    out_specs = P("seq", "head")
    return jax.shard_map(
        per_device, mesh=mesh, in_specs=in_specs, out_specs=out_specs, check_vma=False
    )
```

```python
import jax
import jax.numpy as jnp
from jax import lax
from jax.sharding import PartitionSpec as P

HD = 128
TILE = 128
SEL = 48


def from_behind(value, axis, by):
    count = lax.axis_size(axis)
    return lax.ppermute(value, axis, [(i, (i + by) % count) for i in range(count)])


def pair_grads(query_heads, key_heads, value_heads, grad_heads, norm_rows, delta_rows, admit):
    scale = query_heads.shape[-1] ** (-0.5)
    scores = (
        jnp.einsum("rhd,chd->hrc", query_heads, key_heads, preferred_element_type=jnp.float32)
        * scale
    )
    probs = jnp.where(admit[None], jnp.exp(scores - norm_rows[:, :, None]), 0.0)
    value_grad = jnp.einsum(
        "hrc,rhd->chd", probs.astype(jnp.bfloat16), grad_heads, preferred_element_type=jnp.float32
    )
    prob_grad = jnp.einsum(
        "rhd,chd->hrc", grad_heads, value_heads, preferred_element_type=jnp.float32
    )
    score_grad = (probs * (prob_grad - delta_rows[:, :, None]) * scale).astype(jnp.bfloat16)
    query_grad = jnp.einsum(
        "hrc,chd->rhd", score_grad, key_heads, preferred_element_type=jnp.float32
    )
    key_grad = jnp.einsum(
        "hrc,rhd->chd", score_grad, query_heads, preferred_element_type=jnp.float32
    )
    return (query_grad, key_grad, value_grad)


def settle(total):
    part = lax.optimization_barrier(total.astype(jnp.bfloat16))
    return part.astype(jnp.float32)


def per_device(
    queries,
    keys,
    values,
    attn_out,
    out_grad,
    lse,
    trace_id,
    key_tiles,
    tile_count,
    w_query,
    w_key,
    w_value,
    w_out,
):
    tokens_here, width = queries.shape
    heads_here = width // HD
    seq_count = lax.axis_size("seq")
    seq_index = lax.axis_index("seq")
    tiles_here = tokens_here // TILE
    head_count = lax.axis_size("head")
    head_index = lax.axis_index("head")
    grad_blocks = [out_grad] + [from_behind(out_grad, "head", shift) for shift in range(1, head_count)]
    block_order = (head_index - jnp.arange(head_count)) % head_count
    block_width = out_grad.shape[1]
    w_out_blocks = jnp.take(
        w_out.reshape(w_out.shape[0], head_count, block_width), block_order, axis=1
    ).reshape(w_out.shape[0], head_count * block_width)
    d_attn = lax.dot_general(
        jnp.concatenate(grad_blocks, axis=1),
        w_out_blocks,
        (((1,), (1,)), ((), ())),
        preferred_element_type=jnp.float32,
    ).astype(jnp.bfloat16)
    product = d_attn.astype(jnp.float32) * attn_out.astype(jnp.float32)
    delta = jnp.sum(product.reshape(tokens_here, heads_here, HD), axis=2).T
    query_heads = queries.reshape(tokens_here, heads_here, HD)
    key_heads = keys.reshape(tokens_here, heads_here, HD)
    value_heads = values.reshape(tokens_here, heads_here, HD)
    grad_heads = d_attn.reshape(tokens_here, heads_here, HD)
    trace_here = lax.dynamic_slice_in_dim(trace_id, seq_index * tokens_here, tokens_here, 0)
    slots = jnp.arange(SEL)[None, :] < tile_count[:, None]
    tile_range = jnp.arange(seq_count * tiles_here)
    allowed = jnp.any(
        (key_tiles[:, :, None] == tile_range[None, None, :]) & slots[:, :, None], axis=1
    )

    def visit(key_block, value_block, first_tile):
        block_tiles = key_block.shape[0] // TILE
        listed = lax.dynamic_slice(allowed, (0, first_tile), (tiles_here, block_tiles))
        trace_keys = lax.dynamic_slice_in_dim(trace_id, first_tile * TILE, key_block.shape[0], 0)
        admit = jnp.repeat(jnp.repeat(listed, TILE, axis=0), TILE, axis=1) & (
            trace_here[:, None] != trace_keys[None, :]
        )
        return pair_grads(query_heads, key_block, value_block, grad_heads, lse, delta, admit)

    kv_all = lax.all_gather(jnp.stack([key_heads, value_heads]), "seq", axis=1, tiled=True)
    total_tokens = kv_all.shape[1]
    chunk = min(total_tokens, 2048)
    query_sum = None
    key_parts, value_parts = [], []
    for first in range(0, total_tokens, chunk):
        query_add, key_add, value_add = visit(
            kv_all[0, first:first + chunk], kv_all[1, first:first + chunk], first // TILE
        )
        query_sum = query_add if query_sum is None else query_sum + query_add
        key_parts.append(key_add)
        value_parts.append(value_add)
    parts = jnp.stack([jnp.concatenate(key_parts), jnp.concatenate(value_parts)])
    parts = parts.astype(jnp.bfloat16).reshape((2, seq_count, tokens_here) + parts.shape[2:])
    sums = lax.all_to_all(parts, "seq", 1, 1, tiled=False).astype(jnp.float32).sum(axis=1)
    key_sum, value_sum = (sums[0], sums[1])
    d_query = query_sum.astype(jnp.bfloat16).reshape(tokens_here, width)
    d_key = key_sum.astype(jnp.bfloat16).reshape(tokens_here, width)
    d_value = value_sum.astype(jnp.bfloat16).reshape(tokens_here, width)
    contract = (((1,), (1,)), ((), ()))
    total = lax.dot_general(w_query, d_query, contract, preferred_element_type=jnp.float32)
    total = total + lax.dot_general(w_key, d_key, contract, preferred_element_type=jnp.float32)
    total = total + lax.dot_general(w_value, d_value, contract, preferred_element_type=jnp.float32)
    total = total.reshape((head_count, total.shape[0] // head_count) + total.shape[1:])
    d_input = lax.all_to_all(total, "head", 0, 0, tiled=False).sum(axis=0)
    return d_input.T.astype(jnp.bfloat16)


def solution(mesh):
    in_specs = (
        P("seq", "head"),
        P("seq", "head"),
        P("seq", "head"),
        P("seq", "head"),
        P("seq", "head"),
        P("head", "seq"),
        P(),
        P("seq", None),
        P("seq"),
        P(None, "head"),
        P(None, "head"),
        P(None, "head"),
        P("head", None),
    )
    out_specs = P("seq", "head")
    return jax.shard_map(
        per_device, mesh=mesh, in_specs=in_specs, out_specs=out_specs, check_vma=False
    )
```

```python
import jax
import jax.numpy as jnp
from jax import lax
from jax.sharding import PartitionSpec as P

HD = 128
TILE = 128
SEL = 48


def from_behind(value, axis, by):
    count = lax.axis_size(axis)
    return lax.ppermute(value, axis, [(i, (i + by) % count) for i in range(count)])


def pair_grads(query_heads, key_heads, value_heads, grad_heads, norm_rows, delta_rows, admit):
    scale = query_heads.shape[-1] ** (-0.5)
    scores = (
        jnp.einsum("rhd,chd->hrc", query_heads, key_heads, preferred_element_type=jnp.float32)
        * scale
    )
    probs = jnp.where(admit[None], jnp.exp(scores - norm_rows[:, :, None]), 0.0)
    value_grad = jnp.einsum(
        "hrc,rhd->chd", probs.astype(jnp.bfloat16), grad_heads, preferred_element_type=jnp.float32
    )
    prob_grad = jnp.einsum(
        "rhd,chd->hrc", grad_heads, value_heads, preferred_element_type=jnp.float32
    )
    score_grad = (probs * (prob_grad - delta_rows[:, :, None]) * scale).astype(jnp.bfloat16)
    query_grad = jnp.einsum(
        "hrc,chd->rhd", score_grad, key_heads, preferred_element_type=jnp.float32
    )
    key_grad = jnp.einsum(
        "hrc,rhd->chd", score_grad, query_heads, preferred_element_type=jnp.float32
    )
    return (query_grad, key_grad, value_grad)


def settle(total):
    part = lax.optimization_barrier(total.astype(jnp.bfloat16))
    return part.astype(jnp.float32)


def per_device(
    queries,
    keys,
    values,
    attn_out,
    out_grad,
    lse,
    trace_id,
    key_tiles,
    tile_count,
    w_query,
    w_key,
    w_value,
    w_out,
):
    tokens_here, width = queries.shape
    heads_here = width // HD
    seq_count = lax.axis_size("seq")
    seq_index = lax.axis_index("seq")
    tiles_here = tokens_here // TILE
    head_count = lax.axis_size("head")
    head_index = lax.axis_index("head")
    grad_blocks = [out_grad] + [from_behind(out_grad, "head", shift) for shift in range(1, head_count)]
    block_order = (head_index - jnp.arange(head_count)) % head_count
    block_width = out_grad.shape[1]
    w_out_blocks = jnp.take(
        w_out.reshape(w_out.shape[0], head_count, block_width), block_order, axis=1
    ).reshape(w_out.shape[0], head_count * block_width)
    d_attn = lax.dot_general(
        jnp.concatenate(grad_blocks, axis=1),
        w_out_blocks,
        (((1,), (1,)), ((), ())),
        preferred_element_type=jnp.float32,
    ).astype(jnp.bfloat16)
    product = d_attn.astype(jnp.float32) * attn_out.astype(jnp.float32)
    delta = jnp.sum(product.reshape(tokens_here, heads_here, HD), axis=2).T
    query_heads = queries.reshape(tokens_here, heads_here, HD)
    key_heads = keys.reshape(tokens_here, heads_here, HD)
    value_heads = values.reshape(tokens_here, heads_here, HD)
    grad_heads = d_attn.reshape(tokens_here, heads_here, HD)
    trace_here = lax.dynamic_slice_in_dim(trace_id, seq_index * tokens_here, tokens_here, 0)
    slots = jnp.arange(SEL)[None, :] < tile_count[:, None]
    tile_range = jnp.arange(seq_count * tiles_here)
    allowed = jnp.any(
        (key_tiles[:, :, None] == tile_range[None, None, :]) & slots[:, :, None], axis=1
    )

    kv_all = lax.all_gather(jnp.stack([key_heads, value_heads]), "seq", axis=1, tiled=True)
    tile_total = kv_all.shape[1] // TILE
    kv_tiles = kv_all.reshape((2, tile_total, TILE) + kv_all.shape[2:])
    trace_tiles = trace_id.reshape(tile_total, TILE)
    tile_ids = jnp.arange(tile_total)
    query_rows = []
    key_sum = None
    value_sum = None
    for row in range(tiles_here):
        rows = slice(row * TILE, (row + 1) * TILE)
        listed = key_tiles[row]
        key_block = kv_tiles[0][listed].reshape((SEL * TILE,) + kv_all.shape[2:])
        value_block = kv_tiles[1][listed].reshape((SEL * TILE,) + kv_all.shape[2:])
        used = jnp.repeat(jnp.arange(SEL) < tile_count[row], TILE)
        admit = used[None, :] & (trace_here[rows, None] != trace_tiles[listed].reshape(-1)[None, :])
        query_add, key_add, value_add = pair_grads(
            query_heads[rows], key_block, value_block, grad_heads[rows],
            lse[:, rows], delta[:, rows], admit,
        )
        query_rows.append(query_add)
        onehot = (listed[:, None] == tile_ids[None, :]).astype(jnp.bfloat16)
        spread = (((0,), (0,)), ((), ()))
        key_add = lax.dot_general(
            onehot, key_add.reshape((SEL, -1)).astype(jnp.bfloat16), spread,
            preferred_element_type=jnp.float32,
        )
        value_add = lax.dot_general(
            onehot, value_add.reshape((SEL, -1)).astype(jnp.bfloat16), spread,
            preferred_element_type=jnp.float32,
        )
        key_sum = key_add if key_sum is None else key_sum + key_add
        value_sum = value_add if value_sum is None else value_sum + value_add
    query_sum = jnp.concatenate(query_rows)
    part_shape = (seq_count * tokens_here,) + kv_all.shape[2:]
    key_sum = lax.psum_scatter(key_sum.reshape(part_shape), "seq", scatter_dimension=0, tiled=True)
    value_parts = value_sum.astype(jnp.bfloat16).reshape((seq_count, tokens_here) + kv_all.shape[2:])
    value_sum = lax.all_to_all(value_parts, "seq", 0, 0, tiled=False).astype(jnp.float32).sum(axis=0)
    d_query = query_sum.astype(jnp.bfloat16).reshape(tokens_here, width)
    d_key = key_sum.astype(jnp.bfloat16).reshape(tokens_here, width)
    d_value = value_sum.astype(jnp.bfloat16).reshape(tokens_here, width)
    contract = (((1,), (1,)), ((), ()))
    total = lax.dot_general(w_query, d_query, contract, preferred_element_type=jnp.float32)
    total = total + lax.dot_general(w_key, d_key, contract, preferred_element_type=jnp.float32)
    total = total + lax.dot_general(w_value, d_value, contract, preferred_element_type=jnp.float32)
    total = total.reshape((head_count, total.shape[0] // head_count) + total.shape[1:])
    d_input = lax.all_to_all(total, "head", 0, 0, tiled=False).sum(axis=0)
    return d_input.T.astype(jnp.bfloat16)


def solution(mesh):
    in_specs = (
        P("seq", "head"),
        P("seq", "head"),
        P("seq", "head"),
        P("seq", "head"),
        P("seq", "head"),
        P("head", "seq"),
        P(),
        P("seq", None),
        P("seq"),
        P(None, "head"),
        P(None, "head"),
        P(None, "head"),
        P("head", None),
    )
    out_specs = P("seq", "head")
    return jax.shard_map(
        per_device, mesh=mesh, in_specs=in_specs, out_specs=out_specs, check_vma=False
    )
```

```python
import jax
import jax.numpy as jnp
from jax import lax
from jax.sharding import PartitionSpec as P

HD = 128
TILE = 128
SEL = 48


def from_behind(value, axis, by):
    count = lax.axis_size(axis)
    return lax.ppermute(value, axis, [(i, (i + by) % count) for i in range(count)])


def pair_grads(query_heads, key_heads, value_heads, grad_heads, norm_rows, delta_rows, admit):
    scale = query_heads.shape[-1] ** (-0.5)
    scores = (
        jnp.einsum("rhd,chd->hrc", query_heads, key_heads, preferred_element_type=jnp.float32)
        * scale
    )
    probs = jnp.where(admit[None], jnp.exp(scores - norm_rows[:, :, None]), 0.0)
    value_grad = jnp.einsum(
        "hrc,rhd->chd", probs.astype(jnp.bfloat16), grad_heads, preferred_element_type=jnp.float32
    )
    prob_grad = jnp.einsum(
        "rhd,chd->hrc", grad_heads, value_heads, preferred_element_type=jnp.float32
    )
    score_grad = (probs * (prob_grad - delta_rows[:, :, None]) * scale).astype(jnp.bfloat16)
    query_grad = jnp.einsum(
        "hrc,chd->rhd", score_grad, key_heads, preferred_element_type=jnp.float32
    )
    key_grad = jnp.einsum(
        "hrc,rhd->chd", score_grad, query_heads, preferred_element_type=jnp.float32
    )
    return (query_grad, key_grad, value_grad)


def settle(total):
    part = lax.optimization_barrier(total.astype(jnp.bfloat16))
    return part.astype(jnp.float32)


def per_device(
    queries,
    keys,
    values,
    attn_out,
    out_grad,
    lse,
    trace_id,
    key_tiles,
    tile_count,
    w_query,
    w_key,
    w_value,
    w_out,
):
    tokens_here, width = queries.shape
    heads_here = width // HD
    seq_count = lax.axis_size("seq")
    seq_index = lax.axis_index("seq")
    tiles_here = tokens_here // TILE
    head_count = lax.axis_size("head")
    head_index = lax.axis_index("head")
    grad_blocks = [out_grad] + [from_behind(out_grad, "head", shift) for shift in range(1, head_count)]
    block_order = (head_index - jnp.arange(head_count)) % head_count
    block_width = out_grad.shape[1]
    w_out_blocks = jnp.take(
        w_out.reshape(w_out.shape[0], head_count, block_width), block_order, axis=1
    ).reshape(w_out.shape[0], head_count * block_width)
    d_attn = lax.dot_general(
        jnp.concatenate(grad_blocks, axis=1),
        w_out_blocks,
        (((1,), (1,)), ((), ())),
        preferred_element_type=jnp.float32,
    ).astype(jnp.bfloat16)
    product = d_attn.astype(jnp.float32) * attn_out.astype(jnp.float32)
    delta = jnp.sum(product.reshape(tokens_here, heads_here, HD), axis=2).T
    query_heads = queries.reshape(tokens_here, heads_here, HD)
    key_heads = keys.reshape(tokens_here, heads_here, HD)
    value_heads = values.reshape(tokens_here, heads_here, HD)
    grad_heads = d_attn.reshape(tokens_here, heads_here, HD)
    trace_here = lax.dynamic_slice_in_dim(trace_id, seq_index * tokens_here, tokens_here, 0)
    slots = jnp.arange(SEL)[None, :] < tile_count[:, None]
    tile_range = jnp.arange(seq_count * tiles_here)
    allowed = jnp.any(
        (key_tiles[:, :, None] == tile_range[None, None, :]) & slots[:, :, None], axis=1
    )

    kv_all = lax.all_gather(jnp.stack([key_heads, value_heads]), "seq", axis=1, tiled=True)
    chunks = 8
    width_here = tokens_here // chunks
    kv_split = kv_all.reshape((2, seq_count, chunks, width_here) + kv_all.shape[2:])
    trace_split = trace_id.reshape(seq_count, chunks, width_here)
    allowed_split = allowed.reshape(tiles_here, seq_count, tiles_here)
    query_sum = None
    sum_parts = []
    for part in range(chunks):
        key_block = kv_split[0, :, part].reshape((seq_count * width_here,) + kv_all.shape[2:])
        value_block = kv_split[1, :, part].reshape((seq_count * width_here,) + kv_all.shape[2:])
        listed = allowed_split[:, :, (part * width_here) // TILE]
        admit = jnp.repeat(jnp.repeat(listed, TILE, axis=0), width_here, axis=1) & (
            trace_here[:, None] != trace_split[:, part].reshape(-1)[None, :]
        )
        query_add, key_add, value_add = pair_grads(
            query_heads, key_block, value_block, grad_heads, lse, delta, admit
        )
        query_sum = query_add if query_sum is None else query_sum + query_add
        parts = jnp.stack([key_add, value_add]).astype(jnp.bfloat16)
        parts = parts.reshape((2, seq_count, width_here) + kv_all.shape[2:])
        got = lax.all_to_all(parts, "seq", 1, 1, tiled=False)
        sum_parts.append(got.astype(jnp.float32).sum(axis=1))
    sums = jnp.concatenate(sum_parts, axis=1)
    key_sum, value_sum = (sums[0], sums[1])
    d_query = query_sum.astype(jnp.bfloat16).reshape(tokens_here, width)
    d_key = key_sum.astype(jnp.bfloat16).reshape(tokens_here, width)
    d_value = value_sum.astype(jnp.bfloat16).reshape(tokens_here, width)
    contract = (((1,), (1,)), ((), ()))
    total = lax.dot_general(w_query, d_query, contract, preferred_element_type=jnp.float32)
    total = total + lax.dot_general(w_key, d_key, contract, preferred_element_type=jnp.float32)
    total = total + lax.dot_general(w_value, d_value, contract, preferred_element_type=jnp.float32)
    total = total.reshape((head_count, total.shape[0] // head_count) + total.shape[1:])
    d_input = lax.all_to_all(total, "head", 0, 0, tiled=False).sum(axis=0)
    return d_input.T.astype(jnp.bfloat16)


def solution(mesh):
    in_specs = (
        P("seq", "head"),
        P("seq", "head"),
        P("seq", "head"),
        P("seq", "head"),
        P("seq", "head"),
        P("head", "seq"),
        P(),
        P("seq", None),
        P("seq"),
        P(None, "head"),
        P(None, "head"),
        P(None, "head"),
        P("head", None),
    )
    out_specs = P("seq", "head")
    return jax.shard_map(
        per_device, mesh=mesh, in_specs=in_specs, out_specs=out_specs, check_vma=False
    )
```

```python
import jax
import jax.numpy as jnp
from jax import lax
from jax.sharding import PartitionSpec as P

HD = 128
TILE = 128
SEL = 48


def from_behind(value, axis, by):
    count = lax.axis_size(axis)
    return lax.ppermute(value, axis, [(i, (i + by) % count) for i in range(count)])


def pair_grads(query_heads, key_heads, value_heads, grad_heads, norm_rows, delta_rows, admit):
    scale = query_heads.shape[-1] ** (-0.5)
    scores = (
        jnp.einsum("rhd,chd->hrc", query_heads, key_heads, preferred_element_type=jnp.float32)
        * scale
    )
    probs = jnp.where(admit[None], jnp.exp(scores - norm_rows[:, :, None]), 0.0)
    value_grad = jnp.einsum(
        "hrc,rhd->chd", probs.astype(jnp.bfloat16), grad_heads, preferred_element_type=jnp.float32
    )
    prob_grad = jnp.einsum(
        "rhd,chd->hrc", grad_heads, value_heads, preferred_element_type=jnp.float32
    )
    score_grad = (probs * (prob_grad - delta_rows[:, :, None]) * scale).astype(jnp.bfloat16)
    query_grad = jnp.einsum(
        "hrc,chd->rhd", score_grad, key_heads, preferred_element_type=jnp.float32
    )
    key_grad = jnp.einsum(
        "hrc,rhd->chd", score_grad, query_heads, preferred_element_type=jnp.float32
    )
    return (query_grad, key_grad, value_grad)


def settle(total):
    part = lax.optimization_barrier(total.astype(jnp.bfloat16))
    return part.astype(jnp.float32)


def per_device(
    queries,
    keys,
    values,
    attn_out,
    out_grad,
    lse,
    trace_id,
    key_tiles,
    tile_count,
    w_query,
    w_key,
    w_value,
    w_out,
):
    tokens_here, width = queries.shape
    heads_here = width // HD
    seq_count = lax.axis_size("seq")
    seq_index = lax.axis_index("seq")
    tiles_here = tokens_here // TILE
    head_count = lax.axis_size("head")
    head_index = lax.axis_index("head")
    grad_blocks = [out_grad] + [from_behind(out_grad, "head", shift) for shift in range(1, head_count)]
    block_order = (head_index - jnp.arange(head_count)) % head_count
    block_width = out_grad.shape[1]
    w_out_blocks = jnp.take(
        w_out.reshape(w_out.shape[0], head_count, block_width), block_order, axis=1
    ).reshape(w_out.shape[0], head_count * block_width)
    d_attn = lax.dot_general(
        jnp.concatenate(grad_blocks, axis=1),
        w_out_blocks,
        (((1,), (1,)), ((), ())),
        preferred_element_type=jnp.float32,
    ).astype(jnp.bfloat16)
    product = d_attn.astype(jnp.float32) * attn_out.astype(jnp.float32)
    delta = jnp.sum(product.reshape(tokens_here, heads_here, HD), axis=2).T
    query_heads = queries.reshape(tokens_here, heads_here, HD)
    key_heads = keys.reshape(tokens_here, heads_here, HD)
    value_heads = values.reshape(tokens_here, heads_here, HD)
    grad_heads = d_attn.reshape(tokens_here, heads_here, HD)
    trace_here = lax.dynamic_slice_in_dim(trace_id, seq_index * tokens_here, tokens_here, 0)
    slots = jnp.arange(SEL)[None, :] < tile_count[:, None]
    tile_range = jnp.arange(seq_count * tiles_here)
    allowed = jnp.any(
        (key_tiles[:, :, None] == tile_range[None, None, :]) & slots[:, :, None], axis=1
    )

    def visit(key_block, value_block, first_tile):
        block_tiles = key_block.shape[0] // TILE
        listed = lax.dynamic_slice(allowed, (0, first_tile), (tiles_here, block_tiles))
        trace_keys = lax.dynamic_slice_in_dim(trace_id, first_tile * TILE, key_block.shape[0], 0)
        admit = jnp.repeat(jnp.repeat(listed, TILE, axis=0), TILE, axis=1) & (
            trace_here[:, None] != trace_keys[None, :]
        )
        return pair_grads(query_heads, key_block, value_block, grad_heads, lse, delta, admit)

    kv_all = lax.all_gather(jnp.stack([key_heads, value_heads]), "seq", axis=1, tiled=True)
    total_tokens = kv_all.shape[1]
    chunk = min(total_tokens, 2048)
    query_sum = None
    key_parts, value_parts = [], []
    for first in range(0, total_tokens, chunk):
        query_add, key_add, value_add = visit(
            kv_all[0, first:first + chunk], kv_all[1, first:first + chunk], first // TILE
        )
        query_sum = query_add if query_sum is None else query_sum + query_add
        key_parts.append(key_add)
        value_parts.append(value_add)
    parts = jnp.stack([jnp.concatenate(key_parts), jnp.concatenate(value_parts)])
    parts = parts.astype(jnp.bfloat16).reshape((2, seq_count, tokens_here) + parts.shape[2:])
    sums = lax.all_to_all(parts, "seq", 1, 1, tiled=False).astype(jnp.float32).sum(axis=1)
    key_sum, value_sum = (sums[0], sums[1])
    d_query = query_sum.astype(jnp.bfloat16).reshape(tokens_here, width)
    d_key = key_sum.astype(jnp.bfloat16).reshape(tokens_here, width)
    d_value = value_sum.astype(jnp.bfloat16).reshape(tokens_here, width)
    contract = (((1,), (1,)), ((), ()))
    total = lax.dot_general(w_query, d_query, contract, preferred_element_type=jnp.float32)
    total = total + lax.dot_general(w_key, d_key, contract, preferred_element_type=jnp.float32)
    total = total + lax.dot_general(w_value, d_value, contract, preferred_element_type=jnp.float32)
    total = total.reshape((head_count, total.shape[0] // head_count) + total.shape[1:])
    total = total.astype(jnp.bfloat16)
    d_input = lax.all_to_all(total, "head", 0, 0, tiled=False).astype(jnp.float32).sum(axis=0)
    return d_input.T.astype(jnp.bfloat16)


def solution(mesh):
    in_specs = (
        P("seq", "head"),
        P("seq", "head"),
        P("seq", "head"),
        P("seq", "head"),
        P("seq", "head"),
        P("head", "seq"),
        P(),
        P("seq", None),
        P("seq"),
        P(None, "head"),
        P(None, "head"),
        P(None, "head"),
        P("head", None),
    )
    out_specs = P("seq", "head")
    return jax.shard_map(
        per_device, mesh=mesh, in_specs=in_specs, out_specs=out_specs, check_vma=False
    )
```

```python
import jax
import jax.numpy as jnp
from jax import lax
from jax.sharding import PartitionSpec as P

HD = 128
TILE = 128
SEL = 48


def from_behind(value, axis, by):
    count = lax.axis_size(axis)
    return lax.ppermute(value, axis, [(i, (i + by) % count) for i in range(count)])


def pair_grads(query_heads, key_heads, value_heads, grad_heads, norm_rows, delta_rows, admit):
    scale = query_heads.shape[-1] ** (-0.5)
    scores = (
        jnp.einsum("rhd,chd->hrc", query_heads, key_heads, preferred_element_type=jnp.float32)
        * scale
    )
    probs = jnp.where(admit[None], jnp.exp(scores - norm_rows[:, :, None]), 0.0)
    value_grad = jnp.einsum(
        "hrc,rhd->chd", probs.astype(jnp.bfloat16), grad_heads, preferred_element_type=jnp.float32
    )
    prob_grad = jnp.einsum(
        "rhd,chd->hrc", grad_heads, value_heads, preferred_element_type=jnp.float32
    )
    score_grad = (probs * (prob_grad - delta_rows[:, :, None]) * scale).astype(jnp.bfloat16)
    query_grad = jnp.einsum(
        "hrc,chd->rhd", score_grad, key_heads, preferred_element_type=jnp.float32
    )
    key_grad = jnp.einsum(
        "hrc,rhd->chd", score_grad, query_heads, preferred_element_type=jnp.float32
    )
    return (query_grad, key_grad, value_grad)


def settle(total):
    part = lax.optimization_barrier(total.astype(jnp.bfloat16))
    return part.astype(jnp.float32)


def per_device(
    queries,
    keys,
    values,
    attn_out,
    out_grad,
    lse,
    trace_id,
    key_tiles,
    tile_count,
    w_query,
    w_key,
    w_value,
    w_out,
):
    tokens_here, width = queries.shape
    heads_here = width // HD
    seq_count = lax.axis_size("seq")
    seq_index = lax.axis_index("seq")
    tiles_here = tokens_here // TILE
    head_count = lax.axis_size("head")
    head_index = lax.axis_index("head")
    grad_blocks = [out_grad] + [from_behind(out_grad, "head", shift) for shift in range(1, head_count)]
    block_order = (head_index - jnp.arange(head_count)) % head_count
    block_width = out_grad.shape[1]
    w_out_blocks = jnp.take(
        w_out.reshape(w_out.shape[0], head_count, block_width), block_order, axis=1
    ).reshape(w_out.shape[0], head_count * block_width)
    d_attn = lax.dot_general(
        jnp.concatenate(grad_blocks, axis=1),
        w_out_blocks,
        (((1,), (1,)), ((), ())),
        preferred_element_type=jnp.float32,
    ).astype(jnp.bfloat16)
    product = d_attn.astype(jnp.float32) * attn_out.astype(jnp.float32)
    delta = jnp.sum(product.reshape(tokens_here, heads_here, HD), axis=2).T
    query_heads = queries.reshape(tokens_here, heads_here, HD)
    key_heads = keys.reshape(tokens_here, heads_here, HD)
    value_heads = values.reshape(tokens_here, heads_here, HD)
    grad_heads = d_attn.reshape(tokens_here, heads_here, HD)
    trace_here = lax.dynamic_slice_in_dim(trace_id, seq_index * tokens_here, tokens_here, 0)
    slots = jnp.arange(SEL)[None, :] < tile_count[:, None]
    tile_range = jnp.arange(seq_count * tiles_here)
    allowed = jnp.any(
        (key_tiles[:, :, None] == tile_range[None, None, :]) & slots[:, :, None], axis=1
    )

    def visit(key_block, value_block, first_tile):
        block_tiles = key_block.shape[0] // TILE
        listed = lax.dynamic_slice(allowed, (0, first_tile), (tiles_here, block_tiles))
        trace_keys = lax.dynamic_slice_in_dim(trace_id, first_tile * TILE, key_block.shape[0], 0)
        admit = jnp.repeat(jnp.repeat(listed, TILE, axis=0), TILE, axis=1) & (
            trace_here[:, None] != trace_keys[None, :]
        )
        return pair_grads(query_heads, key_block, value_block, grad_heads, lse, delta, admit)

    kv_all = lax.all_gather(jnp.stack([key_heads, value_heads]), "seq", axis=1, tiled=True)
    total_tokens = kv_all.shape[1]
    chunk = min(total_tokens, 2048)
    query_sum = None
    key_parts, value_parts = [], []
    for first in range(0, total_tokens, chunk):
        query_add, key_add, value_add = visit(
            kv_all[0, first:first + chunk], kv_all[1, first:first + chunk], first // TILE
        )
        query_sum = query_add if query_sum is None else query_sum + query_add
        key_parts.append(key_add)
        value_parts.append(value_add)
    parts = jnp.stack([jnp.concatenate(key_parts), jnp.concatenate(value_parts)])
    parts = parts.astype(jnp.bfloat16)
    sums = lax.psum_scatter(parts, "seq", scatter_dimension=1, tiled=True).astype(jnp.float32)
    key_sum, value_sum = (sums[0], sums[1])
    d_query = query_sum.astype(jnp.bfloat16).reshape(tokens_here, width)
    d_key = key_sum.astype(jnp.bfloat16).reshape(tokens_here, width)
    d_value = value_sum.astype(jnp.bfloat16).reshape(tokens_here, width)
    contract = (((1,), (1,)), ((), ()))
    total = lax.dot_general(w_query, d_query, contract, preferred_element_type=jnp.float32)
    total = total + lax.dot_general(w_key, d_key, contract, preferred_element_type=jnp.float32)
    total = total + lax.dot_general(w_value, d_value, contract, preferred_element_type=jnp.float32)
    total = total.reshape((head_count, total.shape[0] // head_count) + total.shape[1:])
    total = total.astype(jnp.bfloat16)
    d_input = lax.all_to_all(total, "head", 0, 0, tiled=False).astype(jnp.float32).sum(axis=0)
    return d_input.T.astype(jnp.bfloat16)


def solution(mesh):
    in_specs = (
        P("seq", "head"),
        P("seq", "head"),
        P("seq", "head"),
        P("seq", "head"),
        P("seq", "head"),
        P("head", "seq"),
        P(),
        P("seq", None),
        P("seq"),
        P(None, "head"),
        P(None, "head"),
        P(None, "head"),
        P("head", None),
    )
    out_specs = P("seq", "head")
    return jax.shard_map(
        per_device, mesh=mesh, in_specs=in_specs, out_specs=out_specs, check_vma=False
    )
```

```python
import jax
import jax.numpy as jnp
from jax import lax
from jax.sharding import PartitionSpec as P

HD = 128
TILE = 128
SEL = 48


def from_behind(value, axis, by):
    count = lax.axis_size(axis)
    return lax.ppermute(value, axis, [(i, (i + by) % count) for i in range(count)])


def pair_grads(query_heads, key_heads, value_heads, grad_heads, norm_rows, delta_rows, admit):
    scale = query_heads.shape[-1] ** (-0.5)
    scores = (
        jnp.einsum("rhd,chd->hrc", query_heads, key_heads, preferred_element_type=jnp.float32)
        * scale
    )
    probs = jnp.where(admit[None], jnp.exp(scores - norm_rows[:, :, None]), 0.0)
    value_grad = jnp.einsum(
        "hrc,rhd->chd", probs.astype(jnp.bfloat16), grad_heads, preferred_element_type=jnp.float32
    )
    prob_grad = jnp.einsum(
        "rhd,chd->hrc", grad_heads, value_heads, preferred_element_type=jnp.float32
    )
    score_grad = (probs * (prob_grad - delta_rows[:, :, None]) * scale).astype(jnp.bfloat16)
    query_grad = jnp.einsum(
        "hrc,chd->rhd", score_grad, key_heads, preferred_element_type=jnp.float32
    )
    key_grad = jnp.einsum(
        "hrc,rhd->chd", score_grad, query_heads, preferred_element_type=jnp.float32
    )
    return (query_grad, key_grad, value_grad)


def query_grads(query_heads, key_heads, value_heads, grad_heads, norm_rows, delta_rows, admit):
    scale = query_heads.shape[-1] ** (-0.5)
    scores = (
        jnp.einsum("rhd,chd->hrc", query_heads, key_heads, preferred_element_type=jnp.float32)
        * scale
    )
    probs = jnp.where(admit[None], jnp.exp(scores - norm_rows[:, :, None]), 0.0)
    prob_grad = jnp.einsum(
        "rhd,chd->hrc", grad_heads, value_heads, preferred_element_type=jnp.float32
    )
    score_grad = (probs * (prob_grad - delta_rows[:, :, None]) * scale).astype(jnp.bfloat16)
    return jnp.einsum("hrc,chd->rhd", score_grad, key_heads, preferred_element_type=jnp.float32)


def key_grads(query_heads, key_heads, value_heads, grad_heads, norm_rows, delta_rows, admit):
    scale = query_heads.shape[-1] ** (-0.5)
    scores = (
        jnp.einsum("rhd,chd->hrc", query_heads, key_heads, preferred_element_type=jnp.float32)
        * scale
    )
    probs = jnp.where(admit[None], jnp.exp(scores - norm_rows[:, :, None]), 0.0)
    value_grad = jnp.einsum(
        "hrc,rhd->chd", probs.astype(jnp.bfloat16), grad_heads, preferred_element_type=jnp.float32
    )
    prob_grad = jnp.einsum(
        "rhd,chd->hrc", grad_heads, value_heads, preferred_element_type=jnp.float32
    )
    score_grad = (probs * (prob_grad - delta_rows[:, :, None]) * scale).astype(jnp.bfloat16)
    key_grad = jnp.einsum(
        "hrc,rhd->chd", score_grad, query_heads, preferred_element_type=jnp.float32
    )
    return (key_grad, value_grad)


def settle(total):
    part = lax.optimization_barrier(total.astype(jnp.bfloat16))
    return part.astype(jnp.float32)


def per_device(
    queries,
    keys,
    values,
    attn_out,
    out_grad,
    lse,
    trace_id,
    key_tiles,
    tile_count,
    w_query,
    w_key,
    w_value,
    w_out,
):
    tokens_here, width = queries.shape
    heads_here = width // HD
    seq_count = lax.axis_size("seq")
    seq_index = lax.axis_index("seq")
    tiles_here = tokens_here // TILE
    head_count = lax.axis_size("head")
    head_index = lax.axis_index("head")
    grad_blocks = [out_grad] + [from_behind(out_grad, "head", shift) for shift in range(1, head_count)]
    block_order = (head_index - jnp.arange(head_count)) % head_count
    block_width = out_grad.shape[1]
    w_out_blocks = jnp.take(
        w_out.reshape(w_out.shape[0], head_count, block_width), block_order, axis=1
    ).reshape(w_out.shape[0], head_count * block_width)
    d_attn = lax.dot_general(
        jnp.concatenate(grad_blocks, axis=1),
        w_out_blocks,
        (((1,), (1,)), ((), ())),
        preferred_element_type=jnp.float32,
    ).astype(jnp.bfloat16)
    product = d_attn.astype(jnp.float32) * attn_out.astype(jnp.float32)
    delta = jnp.sum(product.reshape(tokens_here, heads_here, HD), axis=2).T
    query_heads = queries.reshape(tokens_here, heads_here, HD)
    key_heads = keys.reshape(tokens_here, heads_here, HD)
    value_heads = values.reshape(tokens_here, heads_here, HD)
    grad_heads = d_attn.reshape(tokens_here, heads_here, HD)
    trace_here = lax.dynamic_slice_in_dim(trace_id, seq_index * tokens_here, tokens_here, 0)
    slots = jnp.arange(SEL)[None, :] < tile_count[:, None]
    tile_range = jnp.arange(seq_count * tiles_here)
    allowed = jnp.any(
        (key_tiles[:, :, None] == tile_range[None, None, :]) & slots[:, :, None], axis=1
    )

    qkv_all = lax.all_gather(
        jnp.stack([query_heads, key_heads, value_heads]), "seq", axis=1, tiled=True
    )
    grad_all = lax.all_gather(grad_heads, "seq", axis=0, tiled=True)
    stats = jnp.concatenate(
        [lse, delta, allowed.astype(jnp.float32).reshape(-1, tokens_here)], axis=0
    )
    stats_all = lax.all_gather(stats, "seq", axis=1, tiled=True)
    total_tokens = qkv_all.shape[1]
    lse_all = stats_all[:heads_here]
    delta_all = stats_all[heads_here:2 * heads_here]
    allowed_all = stats_all[2 * heads_here:].reshape(seq_count, tiles_here, -1)
    allowed_all = allowed_all.reshape(seq_count * tiles_here, -1)[:, : seq_count * tiles_here] > 0.5
    chunk = min(total_tokens, 2048)
    query_sum = None
    for first in range(0, total_tokens, chunk):
        listed = allowed[:, first // TILE:(first + chunk) // TILE]
        admit = jnp.repeat(jnp.repeat(listed, TILE, axis=0), TILE, axis=1) & (
            trace_here[:, None] != trace_id[None, first:first + chunk]
        )
        query_add = query_grads(
            query_heads, qkv_all[1, first:first + chunk], qkv_all[2, first:first + chunk],
            grad_heads, lse, delta, admit,
        )
        query_sum = query_add if query_sum is None else query_sum + query_add
    key_sum = None
    mine = seq_index * tiles_here
    for first in range(0, total_tokens, chunk):
        listed = lax.dynamic_slice_in_dim(allowed_all[first // TILE:(first + chunk) // TILE], mine, tiles_here, 1)
        admit = jnp.repeat(jnp.repeat(listed, TILE, axis=0), TILE, axis=1) & (
            trace_id[first:first + chunk, None] != trace_here[None, :]
        )
        key_add, value_add = key_grads(
            qkv_all[0, first:first + chunk], key_heads, value_heads, grad_all[first:first + chunk],
            lse_all[:, first:first + chunk], delta_all[:, first:first + chunk], admit,
        )
        if key_sum is None:
            key_sum, value_sum = key_add, value_add
        else:
            key_sum, value_sum = key_sum + key_add, value_sum + value_add
    d_query = query_sum.astype(jnp.bfloat16).reshape(tokens_here, width)
    d_key = key_sum.astype(jnp.bfloat16).reshape(tokens_here, width)
    d_value = value_sum.astype(jnp.bfloat16).reshape(tokens_here, width)
    contract = (((1,), (1,)), ((), ()))
    total = lax.dot_general(w_query, d_query, contract, preferred_element_type=jnp.float32)
    total = total + lax.dot_general(w_key, d_key, contract, preferred_element_type=jnp.float32)
    total = total + lax.dot_general(w_value, d_value, contract, preferred_element_type=jnp.float32)
    total = total.reshape((head_count, total.shape[0] // head_count) + total.shape[1:])
    total = total.astype(jnp.bfloat16)
    d_input = lax.all_to_all(total, "head", 0, 0, tiled=False).astype(jnp.float32).sum(axis=0)
    return d_input.T.astype(jnp.bfloat16)


def solution(mesh):
    in_specs = (
        P("seq", "head"),
        P("seq", "head"),
        P("seq", "head"),
        P("seq", "head"),
        P("seq", "head"),
        P("head", "seq"),
        P(),
        P("seq", None),
        P("seq"),
        P(None, "head"),
        P(None, "head"),
        P(None, "head"),
        P("head", None),
    )
    out_specs = P("seq", "head")
    return jax.shard_map(
        per_device, mesh=mesh, in_specs=in_specs, out_specs=out_specs, check_vma=False
    )
```

```python
import jax
import jax.numpy as jnp
from jax import lax
from jax.sharding import PartitionSpec as P

HD = 128
TILE = 128
SEL = 48


def from_behind(value, axis, by):
    count = lax.axis_size(axis)
    return lax.ppermute(value, axis, [(i, (i + by) % count) for i in range(count)])


def pair_grads(query_heads, key_heads, value_heads, grad_heads, norm_rows, delta_rows, admit):
    scale = query_heads.shape[-1] ** (-0.5)
    scores = (
        jnp.einsum("rhd,chd->hrc", query_heads, key_heads, preferred_element_type=jnp.float32)
        * scale
    )
    probs = jnp.where(admit[None], jnp.exp(scores - norm_rows[:, :, None]), 0.0)
    value_grad = jnp.einsum(
        "hrc,rhd->chd", probs.astype(jnp.bfloat16), grad_heads, preferred_element_type=jnp.float32
    )
    prob_grad = jnp.einsum(
        "rhd,chd->hrc", grad_heads, value_heads, preferred_element_type=jnp.float32
    )
    score_grad = (probs * (prob_grad - delta_rows[:, :, None]) * scale).astype(jnp.bfloat16)
    query_grad = jnp.einsum(
        "hrc,chd->rhd", score_grad, key_heads, preferred_element_type=jnp.float32
    )
    key_grad = jnp.einsum(
        "hrc,rhd->chd", score_grad, query_heads, preferred_element_type=jnp.float32
    )
    return (query_grad, key_grad, value_grad)


def query_grads(query_heads, key_heads, value_heads, grad_heads, norm_rows, delta_rows, admit):
    scale = query_heads.shape[-1] ** (-0.5)
    scores = (
        jnp.einsum("rhd,chd->hrc", query_heads, key_heads, preferred_element_type=jnp.float32)
        * scale
    )
    probs = jnp.where(admit[None], jnp.exp(scores - norm_rows[:, :, None]), 0.0)
    prob_grad = jnp.einsum(
        "rhd,chd->hrc", grad_heads, value_heads, preferred_element_type=jnp.float32
    )
    score_grad = (probs * (prob_grad - delta_rows[:, :, None]) * scale).astype(jnp.bfloat16)
    return jnp.einsum("hrc,chd->rhd", score_grad, key_heads, preferred_element_type=jnp.float32)


def key_grads(query_heads, key_heads, value_heads, grad_heads, norm_cols, delta_cols, admit):
    scale = query_heads.shape[-1] ** (-0.5)
    scores = (
        jnp.einsum("chd,rhd->hcr", key_heads, query_heads, preferred_element_type=jnp.float32)
        * scale
    )
    probs = jnp.where(admit[None], jnp.exp(scores - norm_cols[:, None, :]), 0.0)
    value_grad = jnp.einsum(
        "hcr,rhd->chd", probs.astype(jnp.bfloat16), grad_heads, preferred_element_type=jnp.float32
    )
    prob_grad = jnp.einsum(
        "chd,rhd->hcr", value_heads, grad_heads, preferred_element_type=jnp.float32
    )
    score_grad = (probs * (prob_grad - delta_cols[:, None, :]) * scale).astype(jnp.bfloat16)
    key_grad = jnp.einsum(
        "hcr,rhd->chd", score_grad, query_heads, preferred_element_type=jnp.float32
    )
    return (key_grad, value_grad)


def settle(total):
    part = lax.optimization_barrier(total.astype(jnp.bfloat16))
    return part.astype(jnp.float32)


def per_device(
    queries,
    keys,
    values,
    attn_out,
    out_grad,
    lse,
    trace_id,
    key_tiles,
    tile_count,
    w_query,
    w_key,
    w_value,
    w_out,
):
    tokens_here, width = queries.shape
    heads_here = width // HD
    seq_count = lax.axis_size("seq")
    seq_index = lax.axis_index("seq")
    tiles_here = tokens_here // TILE
    head_count = lax.axis_size("head")
    head_index = lax.axis_index("head")
    grad_blocks = [out_grad] + [from_behind(out_grad, "head", shift) for shift in range(1, head_count)]
    block_order = (head_index - jnp.arange(head_count)) % head_count
    block_width = out_grad.shape[1]
    w_out_blocks = jnp.take(
        w_out.reshape(w_out.shape[0], head_count, block_width), block_order, axis=1
    ).reshape(w_out.shape[0], head_count * block_width)
    d_attn = lax.dot_general(
        jnp.concatenate(grad_blocks, axis=1),
        w_out_blocks,
        (((1,), (1,)), ((), ())),
        preferred_element_type=jnp.float32,
    ).astype(jnp.bfloat16)
    product = d_attn.astype(jnp.float32) * attn_out.astype(jnp.float32)
    delta = jnp.sum(product.reshape(tokens_here, heads_here, HD), axis=2).T
    query_heads = queries.reshape(tokens_here, heads_here, HD)
    key_heads = keys.reshape(tokens_here, heads_here, HD)
    value_heads = values.reshape(tokens_here, heads_here, HD)
    grad_heads = d_attn.reshape(tokens_here, heads_here, HD)
    trace_here = lax.dynamic_slice_in_dim(trace_id, seq_index * tokens_here, tokens_here, 0)
    slots = jnp.arange(SEL)[None, :] < tile_count[:, None]
    tile_range = jnp.arange(seq_count * tiles_here)
    allowed = jnp.any(
        (key_tiles[:, :, None] == tile_range[None, None, :]) & slots[:, :, None], axis=1
    )

    qkv_all = lax.all_gather(
        jnp.stack([query_heads, key_heads, value_heads]), "seq", axis=1, tiled=True
    )
    grad_all = lax.all_gather(grad_heads, "seq", axis=0, tiled=True)
    stats = jnp.concatenate(
        [lse, delta, allowed.astype(jnp.float32).reshape(-1, tokens_here)], axis=0
    )
    stats_all = lax.all_gather(stats, "seq", axis=1, tiled=True)
    total_tokens = qkv_all.shape[1]
    lse_all = stats_all[:heads_here]
    delta_all = stats_all[heads_here:2 * heads_here]
    allowed_all = stats_all[2 * heads_here:].reshape(seq_count, tiles_here, -1)
    allowed_all = allowed_all.reshape(seq_count * tiles_here, -1)[:, : seq_count * tiles_here] > 0.5
    chunk = min(total_tokens, 2048)
    query_sum = None
    for first in range(0, total_tokens, chunk):
        listed = allowed[:, first // TILE:(first + chunk) // TILE]
        admit = jnp.repeat(jnp.repeat(listed, TILE, axis=0), TILE, axis=1) & (
            trace_here[:, None] != trace_id[None, first:first + chunk]
        )
        query_add = query_grads(
            query_heads, qkv_all[1, first:first + chunk], qkv_all[2, first:first + chunk],
            grad_heads, lse, delta, admit,
        )
        query_sum = query_add if query_sum is None else query_sum + query_add
    key_sum = None
    mine = seq_index * tiles_here
    for first in range(0, total_tokens, chunk):
        listed = lax.dynamic_slice_in_dim(allowed_all[first // TILE:(first + chunk) // TILE], mine, tiles_here, 1)
        admit = jnp.repeat(jnp.repeat(listed.T, TILE, axis=0), TILE, axis=1) & (
            trace_here[:, None] != trace_id[None, first:first + chunk]
        )
        key_add, value_add = key_grads(
            qkv_all[0, first:first + chunk], key_heads, value_heads, grad_all[first:first + chunk],
            lse_all[:, first:first + chunk], delta_all[:, first:first + chunk], admit,
        )
        if key_sum is None:
            key_sum, value_sum = key_add, value_add
        else:
            key_sum, value_sum = key_sum + key_add, value_sum + value_add
    d_query = query_sum.astype(jnp.bfloat16).reshape(tokens_here, width)
    d_key = key_sum.astype(jnp.bfloat16).reshape(tokens_here, width)
    d_value = value_sum.astype(jnp.bfloat16).reshape(tokens_here, width)
    contract = (((1,), (1,)), ((), ()))
    total = lax.dot_general(w_query, d_query, contract, preferred_element_type=jnp.float32)
    total = total + lax.dot_general(w_key, d_key, contract, preferred_element_type=jnp.float32)
    total = total + lax.dot_general(w_value, d_value, contract, preferred_element_type=jnp.float32)
    total = total.reshape((head_count, total.shape[0] // head_count) + total.shape[1:])
    total = total.astype(jnp.bfloat16)
    d_input = lax.all_to_all(total, "head", 0, 0, tiled=False).astype(jnp.float32).sum(axis=0)
    return d_input.T.astype(jnp.bfloat16)


def solution(mesh):
    in_specs = (
        P("seq", "head"),
        P("seq", "head"),
        P("seq", "head"),
        P("seq", "head"),
        P("seq", "head"),
        P("head", "seq"),
        P(),
        P("seq", None),
        P("seq"),
        P(None, "head"),
        P(None, "head"),
        P(None, "head"),
        P("head", None),
    )
    out_specs = P("seq", "head")
    return jax.shard_map(
        per_device, mesh=mesh, in_specs=in_specs, out_specs=out_specs, check_vma=False
    )
```

```python
import jax
import jax.numpy as jnp
from jax import lax
from jax.sharding import PartitionSpec as P

HD = 128
TILE = 128
SEL = 48


def from_behind(value, axis, by):
    count = lax.axis_size(axis)
    return lax.ppermute(value, axis, [(i, (i + by) % count) for i in range(count)])


def pair_grads(query_heads, key_heads, value_heads, grad_heads, norm_rows, delta_rows, admit):
    scale = query_heads.shape[-1] ** (-0.5)
    scores = (
        jnp.einsum("rhd,chd->hrc", query_heads, key_heads, preferred_element_type=jnp.float32)
        * scale
    )
    probs = jnp.where(admit[None], jnp.exp(scores - norm_rows[:, :, None]), 0.0)
    value_grad = jnp.einsum(
        "hrc,rhd->chd", probs.astype(jnp.bfloat16), grad_heads, preferred_element_type=jnp.float32
    )
    prob_grad = jnp.einsum(
        "rhd,chd->hrc", grad_heads, value_heads, preferred_element_type=jnp.float32
    )
    score_grad = (probs * (prob_grad - delta_rows[:, :, None]) * scale).astype(jnp.bfloat16)
    query_grad = jnp.einsum(
        "hrc,chd->rhd", score_grad, key_heads, preferred_element_type=jnp.float32
    )
    key_grad = jnp.einsum(
        "hrc,rhd->chd", score_grad, query_heads, preferred_element_type=jnp.float32
    )
    return (query_grad, key_grad, value_grad)


def query_grads(query_heads, key_heads, value_heads, grad_heads, norm_rows, delta_rows, admit):
    scale = query_heads.shape[-1] ** (-0.5)
    scores = (
        jnp.einsum("rhd,chd->hrc", query_heads, key_heads, preferred_element_type=jnp.float32)
        * scale
    )
    probs = jnp.where(admit[None], jnp.exp(scores - norm_rows[:, :, None]), 0.0)
    prob_grad = jnp.einsum(
        "rhd,chd->hrc", grad_heads, value_heads, preferred_element_type=jnp.float32
    )
    score_grad = (probs * (prob_grad - delta_rows[:, :, None]) * scale).astype(jnp.bfloat16)
    return jnp.einsum("hrc,chd->rhd", score_grad, key_heads, preferred_element_type=jnp.float32)


def key_grads(query_heads, key_heads, value_heads, grad_heads, norm_cols, delta_cols, admit):
    scale = query_heads.shape[-1] ** (-0.5)
    scores = (
        jnp.einsum("chd,rhd->hcr", key_heads, query_heads, preferred_element_type=jnp.float32)
        * scale
    )
    probs = jnp.where(admit[None], jnp.exp(scores - norm_cols[:, None, :]), 0.0)
    value_grad = jnp.einsum(
        "hcr,rhd->chd", probs.astype(jnp.bfloat16), grad_heads, preferred_element_type=jnp.float32
    )
    prob_grad = jnp.einsum(
        "chd,rhd->hcr", value_heads, grad_heads, preferred_element_type=jnp.float32
    )
    score_grad = (probs * (prob_grad - delta_cols[:, None, :]) * scale).astype(jnp.bfloat16)
    key_grad = jnp.einsum(
        "hcr,rhd->chd", score_grad, query_heads, preferred_element_type=jnp.float32
    )
    return (key_grad, value_grad)


def settle(total):
    part = lax.optimization_barrier(total.astype(jnp.bfloat16))
    return part.astype(jnp.float32)


def per_device(
    queries,
    keys,
    values,
    attn_out,
    out_grad,
    lse,
    trace_id,
    key_tiles,
    tile_count,
    w_query,
    w_key,
    w_value,
    w_out,
):
    tokens_here, width = queries.shape
    heads_here = width // HD
    seq_count = lax.axis_size("seq")
    seq_index = lax.axis_index("seq")
    tiles_here = tokens_here // TILE
    head_count = lax.axis_size("head")
    head_index = lax.axis_index("head")
    grad_blocks = [out_grad] + [from_behind(out_grad, "head", shift) for shift in range(1, head_count)]
    block_order = (head_index - jnp.arange(head_count)) % head_count
    block_width = out_grad.shape[1]
    w_out_blocks = jnp.take(
        w_out.reshape(w_out.shape[0], head_count, block_width), block_order, axis=1
    ).reshape(w_out.shape[0], head_count * block_width)
    d_attn = lax.dot_general(
        jnp.concatenate(grad_blocks, axis=1),
        w_out_blocks,
        (((1,), (1,)), ((), ())),
        preferred_element_type=jnp.float32,
    ).astype(jnp.bfloat16)
    product = d_attn.astype(jnp.float32) * attn_out.astype(jnp.float32)
    delta = jnp.sum(product.reshape(tokens_here, heads_here, HD), axis=2).T
    query_heads = queries.reshape(tokens_here, heads_here, HD)
    key_heads = keys.reshape(tokens_here, heads_here, HD)
    value_heads = values.reshape(tokens_here, heads_here, HD)
    grad_heads = d_attn.reshape(tokens_here, heads_here, HD)
    trace_here = lax.dynamic_slice_in_dim(trace_id, seq_index * tokens_here, tokens_here, 0)
    slots = jnp.arange(SEL)[None, :] < tile_count[:, None]
    tile_range = jnp.arange(seq_count * tiles_here)
    allowed = jnp.any(
        (key_tiles[:, :, None] == tile_range[None, None, :]) & slots[:, :, None], axis=1
    )

    kv_all = lax.all_gather(jnp.stack([key_heads, value_heads]), "seq", axis=1, tiled=True)
    qg_all = lax.all_gather(jnp.stack([query_heads, grad_heads]), "seq", axis=1, tiled=True)
    grad_all = qg_all[1]
    stats = jnp.concatenate(
        [lse, delta, allowed.astype(jnp.float32).reshape(-1, tokens_here)], axis=0
    )
    stats_all = lax.all_gather(stats, "seq", axis=1, tiled=True)
    total_tokens = kv_all.shape[1]
    lse_all = stats_all[:heads_here]
    delta_all = stats_all[heads_here:2 * heads_here]
    allowed_all = stats_all[2 * heads_here:].reshape(seq_count, tiles_here, -1)
    allowed_all = allowed_all.reshape(seq_count * tiles_here, -1)[:, : seq_count * tiles_here] > 0.5
    chunk = min(total_tokens, 2048)
    query_sum = None
    for first in range(0, total_tokens, chunk):
        listed = allowed[:, first // TILE:(first + chunk) // TILE]
        admit = jnp.repeat(jnp.repeat(listed, TILE, axis=0), TILE, axis=1) & (
            trace_here[:, None] != trace_id[None, first:first + chunk]
        )
        query_add = query_grads(
            query_heads, kv_all[0, first:first + chunk], kv_all[1, first:first + chunk],
            grad_heads, lse, delta, admit,
        )
        query_sum = query_add if query_sum is None else query_sum + query_add
    key_sum = None
    mine = seq_index * tiles_here
    for first in range(0, total_tokens, chunk):
        listed = lax.dynamic_slice_in_dim(allowed_all[first // TILE:(first + chunk) // TILE], mine, tiles_here, 1)
        admit = jnp.repeat(jnp.repeat(listed.T, TILE, axis=0), TILE, axis=1) & (
            trace_here[:, None] != trace_id[None, first:first + chunk]
        )
        key_add, value_add = key_grads(
            qg_all[0, first:first + chunk], key_heads, value_heads, grad_all[first:first + chunk],
            lse_all[:, first:first + chunk], delta_all[:, first:first + chunk], admit,
        )
        if key_sum is None:
            key_sum, value_sum = key_add, value_add
        else:
            key_sum, value_sum = key_sum + key_add, value_sum + value_add
    d_query = query_sum.astype(jnp.bfloat16).reshape(tokens_here, width)
    d_key = key_sum.astype(jnp.bfloat16).reshape(tokens_here, width)
    d_value = value_sum.astype(jnp.bfloat16).reshape(tokens_here, width)
    contract = (((1,), (1,)), ((), ()))
    total = lax.dot_general(w_query, d_query, contract, preferred_element_type=jnp.float32)
    total = total + lax.dot_general(w_key, d_key, contract, preferred_element_type=jnp.float32)
    total = total + lax.dot_general(w_value, d_value, contract, preferred_element_type=jnp.float32)
    total = total.reshape((head_count, total.shape[0] // head_count) + total.shape[1:])
    total = total.astype(jnp.bfloat16)
    d_input = lax.all_to_all(total, "head", 0, 0, tiled=False).astype(jnp.float32).sum(axis=0)
    return d_input.T.astype(jnp.bfloat16)


def solution(mesh):
    in_specs = (
        P("seq", "head"),
        P("seq", "head"),
        P("seq", "head"),
        P("seq", "head"),
        P("seq", "head"),
        P("head", "seq"),
        P(),
        P("seq", None),
        P("seq"),
        P(None, "head"),
        P(None, "head"),
        P(None, "head"),
        P("head", None),
    )
    out_specs = P("seq", "head")
    return jax.shard_map(
        per_device, mesh=mesh, in_specs=in_specs, out_specs=out_specs, check_vma=False
    )
```

```python
import jax
import jax.numpy as jnp
from jax import lax
from jax.sharding import PartitionSpec as P

HD = 128
TILE = 128
SEL = 48


def from_behind(value, axis, by):
    count = lax.axis_size(axis)
    return lax.ppermute(value, axis, [(i, (i + by) % count) for i in range(count)])


def pair_grads(query_heads, key_heads, value_heads, grad_heads, norm_rows, delta_rows, admit):
    scale = query_heads.shape[-1] ** (-0.5)
    scores = (
        jnp.einsum("rhd,chd->hrc", query_heads, key_heads, preferred_element_type=jnp.float32)
        * scale
    )
    probs = jnp.where(admit[None], jnp.exp(scores - norm_rows[:, :, None]), 0.0)
    value_grad = jnp.einsum(
        "hrc,rhd->chd", probs.astype(jnp.bfloat16), grad_heads, preferred_element_type=jnp.float32
    )
    prob_grad = jnp.einsum(
        "rhd,chd->hrc", grad_heads, value_heads, preferred_element_type=jnp.float32
    )
    score_grad = (probs * (prob_grad - delta_rows[:, :, None]) * scale).astype(jnp.bfloat16)
    query_grad = jnp.einsum(
        "hrc,chd->rhd", score_grad, key_heads, preferred_element_type=jnp.float32
    )
    key_grad = jnp.einsum(
        "hrc,rhd->chd", score_grad, query_heads, preferred_element_type=jnp.float32
    )
    return (query_grad, key_grad, value_grad)


def query_grads(query_heads, key_heads, value_heads, grad_heads, norm_rows, delta_rows, admit):
    scale = query_heads.shape[-1] ** (-0.5)
    scores = (
        jnp.einsum("rhd,chd->hrc", query_heads, key_heads, preferred_element_type=jnp.float32)
        * scale
    )
    probs = jnp.where(admit[None], jnp.exp(scores - norm_rows[:, :, None]), 0.0)
    prob_grad = jnp.einsum(
        "rhd,chd->hrc", grad_heads, value_heads, preferred_element_type=jnp.float32
    )
    score_grad = (probs * (prob_grad - delta_rows[:, :, None]) * scale).astype(jnp.bfloat16)
    return jnp.einsum("hrc,chd->rhd", score_grad, key_heads, preferred_element_type=jnp.float32)


def key_grads(query_heads, key_heads, value_heads, grad_heads, norm_cols, delta_cols, admit):
    scale = query_heads.shape[-1] ** (-0.5)
    scores = (
        jnp.einsum("chd,rhd->hcr", key_heads, query_heads, preferred_element_type=jnp.float32)
        * scale
    )
    probs = jnp.where(admit[None], jnp.exp(scores - norm_cols[:, None, :]), 0.0)
    value_grad = jnp.einsum(
        "hcr,rhd->chd", probs.astype(jnp.bfloat16), grad_heads, preferred_element_type=jnp.float32
    )
    prob_grad = jnp.einsum(
        "chd,rhd->hcr", value_heads, grad_heads, preferred_element_type=jnp.float32
    )
    score_grad = (probs * (prob_grad - delta_cols[:, None, :]) * scale).astype(jnp.bfloat16)
    key_grad = jnp.einsum(
        "hcr,rhd->chd", score_grad, query_heads, preferred_element_type=jnp.float32
    )
    return (key_grad, value_grad)


def settle(total):
    part = lax.optimization_barrier(total.astype(jnp.bfloat16))
    return part.astype(jnp.float32)


def per_device(
    queries,
    keys,
    values,
    attn_out,
    out_grad,
    lse,
    trace_id,
    key_tiles,
    tile_count,
    w_query,
    w_key,
    w_value,
    w_out,
):
    tokens_here, width = queries.shape
    heads_here = width // HD
    seq_count = lax.axis_size("seq")
    seq_index = lax.axis_index("seq")
    tiles_here = tokens_here // TILE
    head_count = lax.axis_size("head")
    head_index = lax.axis_index("head")
    grad_blocks = [out_grad] + [from_behind(out_grad, "head", shift) for shift in range(1, head_count)]
    block_order = (head_index - jnp.arange(head_count)) % head_count
    block_width = out_grad.shape[1]
    w_out_blocks = jnp.take(
        w_out.reshape(w_out.shape[0], head_count, block_width), block_order, axis=1
    ).reshape(w_out.shape[0], head_count * block_width)
    d_attn = lax.dot_general(
        jnp.concatenate(grad_blocks, axis=1),
        w_out_blocks,
        (((1,), (1,)), ((), ())),
        preferred_element_type=jnp.float32,
    ).astype(jnp.bfloat16)
    product = d_attn.astype(jnp.float32) * attn_out.astype(jnp.float32)
    delta = jnp.sum(product.reshape(tokens_here, heads_here, HD), axis=2).T
    query_heads = queries.reshape(tokens_here, heads_here, HD)
    key_heads = keys.reshape(tokens_here, heads_here, HD)
    value_heads = values.reshape(tokens_here, heads_here, HD)
    grad_heads = d_attn.reshape(tokens_here, heads_here, HD)
    trace_here = lax.dynamic_slice_in_dim(trace_id, seq_index * tokens_here, tokens_here, 0)
    slots = jnp.arange(SEL)[None, :] < tile_count[:, None]
    tile_range = jnp.arange(seq_count * tiles_here)
    allowed = jnp.any(
        (key_tiles[:, :, None] == tile_range[None, None, :]) & slots[:, :, None], axis=1
    )

    kv_all = lax.all_gather(jnp.stack([key_heads, value_heads]), "seq", axis=1, tiled=True)
    qg_all = lax.all_gather(jnp.stack([query_heads, grad_heads]), "seq", axis=1, tiled=True)
    grad_all = qg_all[1]
    stats = jnp.concatenate(
        [lse, delta, allowed.astype(jnp.float32).reshape(-1, tokens_here)], axis=0
    )
    stats_all = lax.all_gather(stats, "seq", axis=1, tiled=True)
    total_tokens = kv_all.shape[1]
    lse_all = stats_all[:heads_here]
    delta_all = stats_all[heads_here:2 * heads_here]
    allowed_all = stats_all[2 * heads_here:].reshape(seq_count, tiles_here, -1)
    allowed_all = allowed_all.reshape(seq_count * tiles_here, -1)[:, : seq_count * tiles_here] > 0.5
    chunk = min(total_tokens, 2048)
    query_sum = None
    for first in range(0, total_tokens, chunk):
        listed = allowed[:, first // TILE:(first + chunk) // TILE]
        admit = jnp.repeat(jnp.repeat(listed, TILE, axis=0), TILE, axis=1) & (
            trace_here[:, None] != trace_id[None, first:first + chunk]
        )
        query_add = query_grads(
            query_heads, kv_all[0, first:first + chunk], kv_all[1, first:first + chunk],
            grad_heads, lse, delta, admit,
        )
        query_sum = query_add if query_sum is None else query_sum + query_add
    key_sum = None
    mine = seq_index * tiles_here
    chunk = min(total_tokens, 4096)
    for first in range(0, total_tokens, chunk):
        listed = lax.dynamic_slice_in_dim(allowed_all[first // TILE:(first + chunk) // TILE], mine, tiles_here, 1)
        admit = jnp.repeat(jnp.repeat(listed.T, TILE, axis=0), TILE, axis=1) & (
            trace_here[:, None] != trace_id[None, first:first + chunk]
        )
        key_add, value_add = key_grads(
            qg_all[0, first:first + chunk], key_heads, value_heads, grad_all[first:first + chunk],
            lse_all[:, first:first + chunk], delta_all[:, first:first + chunk], admit,
        )
        if key_sum is None:
            key_sum, value_sum = key_add, value_add
        else:
            key_sum, value_sum = key_sum + key_add, value_sum + value_add
    d_query = query_sum.astype(jnp.bfloat16).reshape(tokens_here, width)
    d_key = key_sum.astype(jnp.bfloat16).reshape(tokens_here, width)
    d_value = value_sum.astype(jnp.bfloat16).reshape(tokens_here, width)
    contract = (((1,), (1,)), ((), ()))
    total = lax.dot_general(w_query, d_query, contract, preferred_element_type=jnp.float32)
    total = total + lax.dot_general(w_key, d_key, contract, preferred_element_type=jnp.float32)
    total = total + lax.dot_general(w_value, d_value, contract, preferred_element_type=jnp.float32)
    total = total.reshape((head_count, total.shape[0] // head_count) + total.shape[1:])
    total = total.astype(jnp.bfloat16)
    d_input = lax.all_to_all(total, "head", 0, 0, tiled=False).astype(jnp.float32).sum(axis=0)
    return d_input.T.astype(jnp.bfloat16)


def solution(mesh):
    in_specs = (
        P("seq", "head"),
        P("seq", "head"),
        P("seq", "head"),
        P("seq", "head"),
        P("seq", "head"),
        P("head", "seq"),
        P(),
        P("seq", None),
        P("seq"),
        P(None, "head"),
        P(None, "head"),
        P(None, "head"),
        P("head", None),
    )
    out_specs = P("seq", "head")
    return jax.shard_map(
        per_device, mesh=mesh, in_specs=in_specs, out_specs=out_specs, check_vma=False
    )
```

```python
import jax
import jax.numpy as jnp
from jax import lax
from jax.sharding import PartitionSpec as P

HD = 128
TILE = 128
SEL = 48


def from_behind(value, axis, by):
    count = lax.axis_size(axis)
    return lax.ppermute(value, axis, [(i, (i + by) % count) for i in range(count)])


def pair_grads(query_heads, key_heads, value_heads, grad_heads, norm_rows, delta_rows, admit):
    scale = query_heads.shape[-1] ** (-0.5)
    scores = (
        jnp.einsum("rhd,chd->hrc", query_heads, key_heads, preferred_element_type=jnp.float32)
        * scale
    )
    probs = jnp.where(admit[None], jnp.exp(scores - norm_rows[:, :, None]), 0.0)
    value_grad = jnp.einsum(
        "hrc,rhd->chd", probs.astype(jnp.bfloat16), grad_heads, preferred_element_type=jnp.float32
    )
    prob_grad = jnp.einsum(
        "rhd,chd->hrc", grad_heads, value_heads, preferred_element_type=jnp.float32
    )
    score_grad = (probs * (prob_grad - delta_rows[:, :, None]) * scale).astype(jnp.bfloat16)
    query_grad = jnp.einsum(
        "hrc,chd->rhd", score_grad, key_heads, preferred_element_type=jnp.float32
    )
    key_grad = jnp.einsum(
        "hrc,rhd->chd", score_grad, query_heads, preferred_element_type=jnp.float32
    )
    return (query_grad, key_grad, value_grad)


def query_grads(query_heads, key_heads, value_heads, grad_heads, norm_rows, delta_rows, admit):
    scale = query_heads.shape[-1] ** (-0.5)
    scores = (
        jnp.einsum("rhd,chd->hrc", query_heads, key_heads, preferred_element_type=jnp.float32)
        * scale
    )
    probs = jnp.where(admit[None], jnp.exp(scores - norm_rows[:, :, None]), 0.0)
    prob_grad = jnp.einsum(
        "rhd,chd->hrc", grad_heads, value_heads, preferred_element_type=jnp.float32
    )
    score_grad = (probs * (prob_grad - delta_rows[:, :, None]) * scale).astype(jnp.bfloat16)
    return jnp.einsum("hrc,chd->rhd", score_grad, key_heads, preferred_element_type=jnp.float32)


def key_grads(query_heads, key_heads, value_heads, grad_heads, norm_cols, delta_cols, admit):
    scale = query_heads.shape[-1] ** (-0.5)
    scores = (
        jnp.einsum("chd,rhd->hcr", key_heads, query_heads, preferred_element_type=jnp.float32)
        * scale
    )
    probs = jnp.where(admit[None], jnp.exp(scores - norm_cols[:, None, :]), 0.0)
    value_grad = jnp.einsum(
        "hcr,rhd->chd", probs.astype(jnp.bfloat16), grad_heads, preferred_element_type=jnp.float32
    )
    prob_grad = jnp.einsum(
        "chd,rhd->hcr", value_heads, grad_heads, preferred_element_type=jnp.float32
    )
    score_grad = (probs * (prob_grad - delta_cols[:, None, :]) * scale).astype(jnp.bfloat16)
    key_grad = jnp.einsum(
        "hcr,rhd->chd", score_grad, query_heads, preferred_element_type=jnp.float32
    )
    return (key_grad, value_grad)


def settle(total):
    part = lax.optimization_barrier(total.astype(jnp.bfloat16))
    return part.astype(jnp.float32)


def per_device(
    queries,
    keys,
    values,
    attn_out,
    out_grad,
    lse,
    trace_id,
    key_tiles,
    tile_count,
    w_query,
    w_key,
    w_value,
    w_out,
):
    tokens_here, width = queries.shape
    heads_here = width // HD
    seq_count = lax.axis_size("seq")
    seq_index = lax.axis_index("seq")
    tiles_here = tokens_here // TILE
    head_count = lax.axis_size("head")
    head_index = lax.axis_index("head")
    grad_blocks = [out_grad] + [from_behind(out_grad, "head", shift) for shift in range(1, head_count)]
    block_order = (head_index - jnp.arange(head_count)) % head_count
    block_width = out_grad.shape[1]
    w_out_blocks = jnp.take(
        w_out.reshape(w_out.shape[0], head_count, block_width), block_order, axis=1
    ).reshape(w_out.shape[0], head_count * block_width)
    d_attn = lax.dot_general(
        jnp.concatenate(grad_blocks, axis=1),
        w_out_blocks,
        (((1,), (1,)), ((), ())),
        preferred_element_type=jnp.float32,
    ).astype(jnp.bfloat16)
    product = d_attn.astype(jnp.float32) * attn_out.astype(jnp.float32)
    delta = jnp.sum(product.reshape(tokens_here, heads_here, HD), axis=2).T
    query_heads = queries.reshape(tokens_here, heads_here, HD)
    key_heads = keys.reshape(tokens_here, heads_here, HD)
    value_heads = values.reshape(tokens_here, heads_here, HD)
    grad_heads = d_attn.reshape(tokens_here, heads_here, HD)
    trace_here = lax.dynamic_slice_in_dim(trace_id, seq_index * tokens_here, tokens_here, 0)
    slots = jnp.arange(SEL)[None, :] < tile_count[:, None]
    tile_range = jnp.arange(seq_count * tiles_here)
    allowed = jnp.any(
        (key_tiles[:, :, None] == tile_range[None, None, :]) & slots[:, :, None], axis=1
    )

    kv_all = lax.all_gather(jnp.stack([key_heads, value_heads]), "seq", axis=1, tiled=True)
    qg_all = lax.all_gather(jnp.stack([query_heads, grad_heads]), "seq", axis=1, tiled=True)
    grad_all = qg_all[1]
    stats = jnp.concatenate(
        [lse, delta, allowed.astype(jnp.float32).reshape(-1, tokens_here)], axis=0
    )
    stats_all = lax.all_gather(stats, "seq", axis=1, tiled=True)
    total_tokens = kv_all.shape[1]
    lse_all = stats_all[:heads_here]
    delta_all = stats_all[heads_here:2 * heads_here]
    allowed_all = stats_all[2 * heads_here:].reshape(seq_count, tiles_here, -1)
    allowed_all = allowed_all.reshape(seq_count * tiles_here, -1)[:, : seq_count * tiles_here] > 0.5
    chunk = min(total_tokens, 4096)
    query_sum = None
    for first in range(0, total_tokens, chunk):
        listed = allowed[:, first // TILE:(first + chunk) // TILE]
        admit = jnp.repeat(jnp.repeat(listed, TILE, axis=0), TILE, axis=1) & (
            trace_here[:, None] != trace_id[None, first:first + chunk]
        )
        query_add = query_grads(
            query_heads, kv_all[0, first:first + chunk], kv_all[1, first:first + chunk],
            grad_heads, lse, delta, admit,
        )
        query_sum = query_add if query_sum is None else query_sum + query_add
    key_sum = None
    mine = seq_index * tiles_here
    chunk = min(total_tokens, 4096)
    for first in range(0, total_tokens, chunk):
        listed = lax.dynamic_slice_in_dim(allowed_all[first // TILE:(first + chunk) // TILE], mine, tiles_here, 1)
        admit = jnp.repeat(jnp.repeat(listed.T, TILE, axis=0), TILE, axis=1) & (
            trace_here[:, None] != trace_id[None, first:first + chunk]
        )
        key_add, value_add = key_grads(
            qg_all[0, first:first + chunk], key_heads, value_heads, grad_all[first:first + chunk],
            lse_all[:, first:first + chunk], delta_all[:, first:first + chunk], admit,
        )
        if key_sum is None:
            key_sum, value_sum = key_add, value_add
        else:
            key_sum, value_sum = key_sum + key_add, value_sum + value_add
    d_query = query_sum.astype(jnp.bfloat16).reshape(tokens_here, width)
    d_key = key_sum.astype(jnp.bfloat16).reshape(tokens_here, width)
    d_value = value_sum.astype(jnp.bfloat16).reshape(tokens_here, width)
    contract = (((1,), (1,)), ((), ()))
    total = lax.dot_general(w_query, d_query, contract, preferred_element_type=jnp.float32)
    total = total + lax.dot_general(w_key, d_key, contract, preferred_element_type=jnp.float32)
    total = total + lax.dot_general(w_value, d_value, contract, preferred_element_type=jnp.float32)
    total = total.reshape((head_count, total.shape[0] // head_count) + total.shape[1:])
    total = total.astype(jnp.bfloat16)
    d_input = lax.all_to_all(total, "head", 0, 0, tiled=False).astype(jnp.float32).sum(axis=0)
    return d_input.T.astype(jnp.bfloat16)


def solution(mesh):
    in_specs = (
        P("seq", "head"),
        P("seq", "head"),
        P("seq", "head"),
        P("seq", "head"),
        P("seq", "head"),
        P("head", "seq"),
        P(),
        P("seq", None),
        P("seq"),
        P(None, "head"),
        P(None, "head"),
        P(None, "head"),
        P("head", None),
    )
    out_specs = P("seq", "head")
    return jax.shard_map(
        per_device, mesh=mesh, in_specs=in_specs, out_specs=out_specs, check_vma=False
    )
```

```python
import jax
import jax.numpy as jnp
from jax import lax
from jax.sharding import PartitionSpec as P

HD = 128
TILE = 128
SEL = 48


def from_behind(value, axis, by):
    count = lax.axis_size(axis)
    return lax.ppermute(value, axis, [(i, (i + by) % count) for i in range(count)])


def pair_grads(query_heads, key_heads, value_heads, grad_heads, norm_rows, delta_rows, admit):
    scale = query_heads.shape[-1] ** (-0.5)
    scores = (
        jnp.einsum("rhd,chd->hrc", query_heads, key_heads, preferred_element_type=jnp.float32)
        * scale
    )
    probs = jnp.where(admit[None], jnp.exp(scores - norm_rows[:, :, None]), 0.0)
    value_grad = jnp.einsum(
        "hrc,rhd->chd", probs.astype(jnp.bfloat16), grad_heads, preferred_element_type=jnp.float32
    )
    prob_grad = jnp.einsum(
        "rhd,chd->hrc", grad_heads, value_heads, preferred_element_type=jnp.float32
    )
    score_grad = (probs * (prob_grad - delta_rows[:, :, None]) * scale).astype(jnp.bfloat16)
    query_grad = jnp.einsum(
        "hrc,chd->rhd", score_grad, key_heads, preferred_element_type=jnp.float32
    )
    key_grad = jnp.einsum(
        "hrc,rhd->chd", score_grad, query_heads, preferred_element_type=jnp.float32
    )
    return (query_grad, key_grad, value_grad)


def query_grads(query_heads, key_heads, value_heads, grad_heads, norm_rows, delta_rows, admit):
    scale = query_heads.shape[-1] ** (-0.5)
    scores = (
        jnp.einsum("rhd,chd->hrc", query_heads, key_heads, preferred_element_type=jnp.float32)
        * scale
    )
    probs = jnp.where(admit[None], jnp.exp(scores - norm_rows[:, :, None]), 0.0)
    prob_grad = jnp.einsum(
        "rhd,chd->hrc", grad_heads, value_heads, preferred_element_type=jnp.float32
    )
    score_grad = (probs * (prob_grad - delta_rows[:, :, None]) * scale).astype(jnp.bfloat16)
    return jnp.einsum("hrc,chd->rhd", score_grad, key_heads, preferred_element_type=jnp.float32)


def key_grads(query_heads, key_heads, value_heads, grad_heads, norm_cols, delta_cols, admit):
    scale = query_heads.shape[-1] ** (-0.5)
    scores = (
        jnp.einsum("chd,rhd->hcr", key_heads, query_heads, preferred_element_type=jnp.float32)
        * scale
    )
    probs = jnp.where(admit[None], jnp.exp(scores - norm_cols[:, None, :]), 0.0)
    value_grad = jnp.einsum(
        "hcr,rhd->chd", probs.astype(jnp.bfloat16), grad_heads, preferred_element_type=jnp.float32
    )
    prob_grad = jnp.einsum(
        "chd,rhd->hcr", value_heads, grad_heads, preferred_element_type=jnp.float32
    )
    score_grad = (probs * (prob_grad - delta_cols[:, None, :]) * scale).astype(jnp.bfloat16)
    key_grad = jnp.einsum(
        "hcr,rhd->chd", score_grad, query_heads, preferred_element_type=jnp.float32
    )
    return (key_grad, value_grad)


def settle(total):
    part = lax.optimization_barrier(total.astype(jnp.bfloat16))
    return part.astype(jnp.float32)


def per_device(
    queries,
    keys,
    values,
    attn_out,
    out_grad,
    lse,
    trace_id,
    key_tiles,
    tile_count,
    w_query,
    w_key,
    w_value,
    w_out,
):
    tokens_here, width = queries.shape
    heads_here = width // HD
    seq_count = lax.axis_size("seq")
    seq_index = lax.axis_index("seq")
    tiles_here = tokens_here // TILE
    head_count = lax.axis_size("head")
    head_index = lax.axis_index("head")
    grad_blocks = [out_grad] + [from_behind(out_grad, "head", shift) for shift in range(1, head_count)]
    block_order = (head_index - jnp.arange(head_count)) % head_count
    block_width = out_grad.shape[1]
    w_out_blocks = jnp.take(
        w_out.reshape(w_out.shape[0], head_count, block_width), block_order, axis=1
    ).reshape(w_out.shape[0], head_count * block_width)
    d_attn = lax.dot_general(
        jnp.concatenate(grad_blocks, axis=1),
        w_out_blocks,
        (((1,), (1,)), ((), ())),
        preferred_element_type=jnp.float32,
    ).astype(jnp.bfloat16)
    product = d_attn.astype(jnp.float32) * attn_out.astype(jnp.float32)
    delta = jnp.sum(product.reshape(tokens_here, heads_here, HD), axis=2).T
    query_heads = queries.reshape(tokens_here, heads_here, HD)
    key_heads = keys.reshape(tokens_here, heads_here, HD)
    value_heads = values.reshape(tokens_here, heads_here, HD)
    grad_heads = d_attn.reshape(tokens_here, heads_here, HD)
    trace_here = lax.dynamic_slice_in_dim(trace_id, seq_index * tokens_here, tokens_here, 0)
    slots = jnp.arange(SEL)[None, :] < tile_count[:, None]
    tile_range = jnp.arange(seq_count * tiles_here)
    allowed = jnp.any(
        (key_tiles[:, :, None] == tile_range[None, None, :]) & slots[:, :, None], axis=1
    )

    kv_all = lax.all_gather(jnp.stack([key_heads, value_heads]), "seq", axis=1, tiled=True)
    qg_all = lax.all_gather(jnp.stack([query_heads, grad_heads]), "seq", axis=1, tiled=True)
    grad_all = qg_all[1]
    stats = jnp.concatenate(
        [lse, delta, allowed.astype(jnp.float32).reshape(-1, tokens_here)], axis=0
    )
    stats_all = lax.all_gather(stats, "seq", axis=1, tiled=True)
    total_tokens = kv_all.shape[1]
    lse_all = stats_all[:heads_here]
    delta_all = stats_all[heads_here:2 * heads_here]
    allowed_all = stats_all[2 * heads_here:].reshape(seq_count, tiles_here, -1)
    allowed_all = allowed_all.reshape(seq_count * tiles_here, -1)[:, : seq_count * tiles_here] > 0.5
    chunk = min(total_tokens, 4096)
    query_sum = None
    for first in range(0, total_tokens, chunk):
        listed = allowed[:, first // TILE:(first + chunk) // TILE]
        admit = jnp.repeat(jnp.repeat(listed, TILE, axis=0), TILE, axis=1) & (
            trace_here[:, None] != trace_id[None, first:first + chunk]
        )
        query_add = query_grads(
            query_heads, kv_all[0, first:first + chunk], kv_all[1, first:first + chunk],
            grad_heads, lse, delta, admit,
        )
        query_sum = query_add if query_sum is None else query_sum + query_add
    key_sum = None
    mine = seq_index * tiles_here
    chunk = min(total_tokens, 4096)
    for first in range(0, total_tokens, chunk):
        listed = lax.dynamic_slice_in_dim(allowed_all[first // TILE:(first + chunk) // TILE], mine, tiles_here, 1)
        admit = jnp.repeat(jnp.repeat(listed.T, TILE, axis=0), TILE, axis=1) & (
            trace_here[:, None] != trace_id[None, first:first + chunk]
        )
        key_add, value_add = key_grads(
            qg_all[0, first:first + chunk], key_heads, value_heads, grad_all[first:first + chunk],
            lse_all[:, first:first + chunk], delta_all[:, first:first + chunk], admit,
        )
        if key_sum is None:
            key_sum, value_sum = key_add, value_add
        else:
            key_sum, value_sum = key_sum + key_add, value_sum + value_add
    d_query = query_sum.astype(jnp.bfloat16).reshape(tokens_here, width)
    d_key = key_sum.astype(jnp.bfloat16).reshape(tokens_here, width)
    d_value = value_sum.astype(jnp.bfloat16).reshape(tokens_here, width)
    contract = (((1,), (1,)), ((), ()))
    total = lax.dot_general(w_query, d_query, contract, preferred_element_type=jnp.float32)
    total = total + lax.dot_general(w_key, d_key, contract, preferred_element_type=jnp.float32)
    total = total + lax.dot_general(w_value, d_value, contract, preferred_element_type=jnp.float32)
    total = total.reshape((head_count, total.shape[0] // head_count) + total.shape[1:])
    total = total.astype(jnp.bfloat16)
    d_input = lax.dynamic_index_in_dim(total, head_index, 0, keepdims=False).astype(jnp.float32)
    for shift in range(1, head_count):
        owed = lax.dynamic_index_in_dim(total, (head_index + shift) % head_count, 0, keepdims=False)
        d_input = d_input + from_behind(owed, "head", shift).astype(jnp.float32)
    return d_input.T.astype(jnp.bfloat16)


def solution(mesh):
    in_specs = (
        P("seq", "head"),
        P("seq", "head"),
        P("seq", "head"),
        P("seq", "head"),
        P("seq", "head"),
        P("head", "seq"),
        P(),
        P("seq", None),
        P("seq"),
        P(None, "head"),
        P(None, "head"),
        P(None, "head"),
        P("head", None),
    )
    out_specs = P("seq", "head")
    return jax.shard_map(
        per_device, mesh=mesh, in_specs=in_specs, out_specs=out_specs, check_vma=False
    )
```

```python
import jax
import jax.numpy as jnp
from jax import lax
from jax.sharding import PartitionSpec as P

HD = 128
TILE = 128
SEL = 48


def from_behind(value, axis, by):
    count = lax.axis_size(axis)
    return lax.ppermute(value, axis, [(i, (i + by) % count) for i in range(count)])


def pair_grads(query_heads, key_heads, value_heads, grad_heads, norm_rows, delta_rows, admit):
    scale = query_heads.shape[-1] ** (-0.5)
    scores = (
        jnp.einsum("rhd,chd->hrc", query_heads, key_heads, preferred_element_type=jnp.float32)
        * scale
    )
    probs = jnp.where(admit[None], jnp.exp(scores - norm_rows[:, :, None]), 0.0)
    value_grad = jnp.einsum(
        "hrc,rhd->chd", probs.astype(jnp.bfloat16), grad_heads, preferred_element_type=jnp.float32
    )
    prob_grad = jnp.einsum(
        "rhd,chd->hrc", grad_heads, value_heads, preferred_element_type=jnp.float32
    )
    score_grad = (probs * (prob_grad - delta_rows[:, :, None]) * scale).astype(jnp.bfloat16)
    query_grad = jnp.einsum(
        "hrc,chd->rhd", score_grad, key_heads, preferred_element_type=jnp.float32
    )
    key_grad = jnp.einsum(
        "hrc,rhd->chd", score_grad, query_heads, preferred_element_type=jnp.float32
    )
    return (query_grad, key_grad, value_grad)


def query_grads(query_heads, key_heads, value_heads, grad_heads, norm_rows, delta_rows, admit):
    scale = query_heads.shape[-1] ** (-0.5)
    scores = (
        jnp.einsum("rhd,chd->hrc", query_heads, key_heads, preferred_element_type=jnp.float32)
        * scale
    )
    probs = jnp.where(admit[None], jnp.exp(scores - norm_rows[:, :, None]), 0.0)
    prob_grad = jnp.einsum(
        "rhd,chd->hrc", grad_heads, value_heads, preferred_element_type=jnp.float32
    )
    score_grad = (probs * (prob_grad - delta_rows[:, :, None]) * scale).astype(jnp.bfloat16)
    return jnp.einsum("hrc,chd->rhd", score_grad, key_heads, preferred_element_type=jnp.float32)


def key_grads(query_heads, key_heads, value_heads, grad_heads, norm_cols, delta_cols, admit):
    scale = query_heads.shape[-1] ** (-0.5)
    scores = (
        jnp.einsum("chd,rhd->hcr", key_heads, query_heads, preferred_element_type=jnp.float32)
        * scale
    )
    probs = jnp.where(admit[None], jnp.exp(scores - norm_cols[:, None, :]), 0.0)
    value_grad = jnp.einsum(
        "hcr,rhd->chd", probs.astype(jnp.bfloat16), grad_heads, preferred_element_type=jnp.float32
    )
    prob_grad = jnp.einsum(
        "chd,rhd->hcr", value_heads, grad_heads, preferred_element_type=jnp.float32
    )
    score_grad = (probs * (prob_grad - delta_cols[:, None, :]) * scale).astype(jnp.bfloat16)
    key_grad = jnp.einsum(
        "hcr,rhd->chd", score_grad, query_heads, preferred_element_type=jnp.float32
    )
    return (key_grad, value_grad)


def settle(total):
    part = lax.optimization_barrier(total.astype(jnp.bfloat16))
    return part.astype(jnp.float32)


def per_device(
    queries,
    keys,
    values,
    attn_out,
    out_grad,
    lse,
    trace_id,
    key_tiles,
    tile_count,
    w_query,
    w_key,
    w_value,
    w_out,
):
    tokens_here, width = queries.shape
    heads_here = width // HD
    seq_count = lax.axis_size("seq")
    seq_index = lax.axis_index("seq")
    tiles_here = tokens_here // TILE
    head_count = lax.axis_size("head")
    head_index = lax.axis_index("head")
    grad_blocks = [out_grad] + [from_behind(out_grad, "head", shift) for shift in range(1, head_count)]
    block_order = (head_index - jnp.arange(head_count)) % head_count
    block_width = out_grad.shape[1]
    w_out_blocks = jnp.take(
        w_out.reshape(w_out.shape[0], head_count, block_width), block_order, axis=1
    ).reshape(w_out.shape[0], head_count * block_width)
    d_attn = lax.dot_general(
        jnp.concatenate(grad_blocks, axis=1),
        w_out_blocks,
        (((1,), (1,)), ((), ())),
        preferred_element_type=jnp.float32,
    ).astype(jnp.bfloat16)
    product = d_attn.astype(jnp.float32) * attn_out.astype(jnp.float32)
    delta = jnp.sum(product.reshape(tokens_here, heads_here, HD), axis=2).T
    query_heads = queries.reshape(tokens_here, heads_here, HD)
    key_heads = keys.reshape(tokens_here, heads_here, HD)
    value_heads = values.reshape(tokens_here, heads_here, HD)
    grad_heads = d_attn.reshape(tokens_here, heads_here, HD)
    trace_here = lax.dynamic_slice_in_dim(trace_id, seq_index * tokens_here, tokens_here, 0)
    slots = jnp.arange(SEL)[None, :] < tile_count[:, None]
    tile_range = jnp.arange(seq_count * tiles_here)
    allowed = jnp.any(
        (key_tiles[:, :, None] == tile_range[None, None, :]) & slots[:, :, None], axis=1
    )

    kv_all = lax.all_gather(jnp.stack([key_heads, value_heads]), "seq", axis=1, tiled=True)
    qg_all = lax.all_gather(jnp.stack([query_heads, grad_heads]), "seq", axis=1, tiled=True)
    grad_all = qg_all[1]
    stats = jnp.concatenate(
        [lse, delta, allowed.astype(jnp.float32).reshape(-1, tokens_here)], axis=0
    )
    stats_all = lax.all_gather(stats, "seq", axis=1, tiled=True)
    total_tokens = kv_all.shape[1]
    lse_all = stats_all[:heads_here]
    delta_all = stats_all[heads_here:2 * heads_here]
    allowed_all = stats_all[2 * heads_here:].reshape(seq_count, tiles_here, -1)
    allowed_all = allowed_all.reshape(seq_count * tiles_here, -1)[:, : seq_count * tiles_here] > 0.5
    chunk = min(total_tokens, 4096)
    query_sum = None
    for first in range(0, total_tokens, chunk):
        listed = allowed[:, first // TILE:(first + chunk) // TILE]
        admit = jnp.repeat(jnp.repeat(listed, TILE, axis=0), TILE, axis=1) & (
            trace_here[:, None] != trace_id[None, first:first + chunk]
        )
        query_add = query_grads(
            query_heads, kv_all[0, first:first + chunk], kv_all[1, first:first + chunk],
            grad_heads, lse, delta, admit,
        )
        query_sum = query_add if query_sum is None else query_sum + query_add
    key_sum = None
    mine = seq_index * tiles_here
    chunk = min(total_tokens, 8192)
    for first in range(0, total_tokens, chunk):
        listed = lax.dynamic_slice_in_dim(allowed_all[first // TILE:(first + chunk) // TILE], mine, tiles_here, 1)
        admit = jnp.repeat(jnp.repeat(listed.T, TILE, axis=0), TILE, axis=1) & (
            trace_here[:, None] != trace_id[None, first:first + chunk]
        )
        key_add, value_add = key_grads(
            qg_all[0, first:first + chunk], key_heads, value_heads, grad_all[first:first + chunk],
            lse_all[:, first:first + chunk], delta_all[:, first:first + chunk], admit,
        )
        if key_sum is None:
            key_sum, value_sum = key_add, value_add
        else:
            key_sum, value_sum = key_sum + key_add, value_sum + value_add
    d_query = query_sum.astype(jnp.bfloat16).reshape(tokens_here, width)
    d_key = key_sum.astype(jnp.bfloat16).reshape(tokens_here, width)
    d_value = value_sum.astype(jnp.bfloat16).reshape(tokens_here, width)
    contract = (((1,), (1,)), ((), ()))
    total = lax.dot_general(w_query, d_query, contract, preferred_element_type=jnp.float32)
    total = total + lax.dot_general(w_key, d_key, contract, preferred_element_type=jnp.float32)
    total = total + lax.dot_general(w_value, d_value, contract, preferred_element_type=jnp.float32)
    total = total.reshape((head_count, total.shape[0] // head_count) + total.shape[1:])
    total = total.astype(jnp.bfloat16)
    d_input = lax.dynamic_index_in_dim(total, head_index, 0, keepdims=False).astype(jnp.float32)
    for shift in range(1, head_count):
        owed = lax.dynamic_index_in_dim(total, (head_index + shift) % head_count, 0, keepdims=False)
        d_input = d_input + from_behind(owed, "head", shift).astype(jnp.float32)
    return d_input.T.astype(jnp.bfloat16)


def solution(mesh):
    in_specs = (
        P("seq", "head"),
        P("seq", "head"),
        P("seq", "head"),
        P("seq", "head"),
        P("seq", "head"),
        P("head", "seq"),
        P(),
        P("seq", None),
        P("seq"),
        P(None, "head"),
        P(None, "head"),
        P(None, "head"),
        P("head", None),
    )
    out_specs = P("seq", "head")
    return jax.shard_map(
        per_device, mesh=mesh, in_specs=in_specs, out_specs=out_specs, check_vma=False
    )
```

```python
import jax
import jax.numpy as jnp
from jax import lax
from jax.sharding import PartitionSpec as P

HD = 128
TILE = 128
SEL = 48


def from_behind(value, axis, by):
    count = lax.axis_size(axis)
    return lax.ppermute(value, axis, [(i, (i + by) % count) for i in range(count)])


def pair_grads(query_heads, key_heads, value_heads, grad_heads, norm_rows, delta_rows, admit):
    scale = query_heads.shape[-1] ** (-0.5)
    scores = (
        jnp.einsum("rhd,chd->hrc", query_heads, key_heads, preferred_element_type=jnp.float32)
        * scale
    )
    probs = jnp.where(admit[None], jnp.exp(scores - norm_rows[:, :, None]), 0.0)
    value_grad = jnp.einsum(
        "hrc,rhd->chd", probs.astype(jnp.bfloat16), grad_heads, preferred_element_type=jnp.float32
    )
    prob_grad = jnp.einsum(
        "rhd,chd->hrc", grad_heads, value_heads, preferred_element_type=jnp.float32
    )
    score_grad = (probs * (prob_grad - delta_rows[:, :, None]) * scale).astype(jnp.bfloat16)
    query_grad = jnp.einsum(
        "hrc,chd->rhd", score_grad, key_heads, preferred_element_type=jnp.float32
    )
    key_grad = jnp.einsum(
        "hrc,rhd->chd", score_grad, query_heads, preferred_element_type=jnp.float32
    )
    return (query_grad, key_grad, value_grad)


def query_grads(query_heads, key_heads, value_heads, grad_heads, norm_rows, delta_rows, admit):
    scale = query_heads.shape[-1] ** (-0.5)
    scores = (
        jnp.einsum("rhd,chd->hrc", query_heads, key_heads, preferred_element_type=jnp.float32)
        * scale
    )
    probs = jnp.where(admit[None], jnp.exp(scores - norm_rows[:, :, None]), 0.0)
    prob_grad = jnp.einsum(
        "rhd,chd->hrc", grad_heads, value_heads, preferred_element_type=jnp.float32
    )
    score_grad = (probs * (prob_grad - delta_rows[:, :, None]) * scale).astype(jnp.bfloat16)
    return jnp.einsum("hrc,chd->rhd", score_grad, key_heads, preferred_element_type=jnp.float32)


def key_grads(query_heads, key_heads, value_heads, grad_heads, norm_cols, delta_cols, admit):
    scale = query_heads.shape[-1] ** (-0.5)
    scores = (
        jnp.einsum("chd,rhd->hcr", key_heads, query_heads, preferred_element_type=jnp.float32)
        * scale
    )
    probs = jnp.where(admit[None], jnp.exp(scores - norm_cols[:, None, :]), 0.0)
    value_grad = jnp.einsum(
        "hcr,rhd->chd", probs.astype(jnp.bfloat16), grad_heads, preferred_element_type=jnp.float32
    )
    prob_grad = jnp.einsum(
        "chd,rhd->hcr", value_heads, grad_heads, preferred_element_type=jnp.float32
    )
    score_grad = (probs * (prob_grad - delta_cols[:, None, :]) * scale).astype(jnp.bfloat16)
    key_grad = jnp.einsum(
        "hcr,rhd->chd", score_grad, query_heads, preferred_element_type=jnp.float32
    )
    return (key_grad, value_grad)


def settle(total):
    part = lax.optimization_barrier(total.astype(jnp.bfloat16))
    return part.astype(jnp.float32)


def per_device(
    queries,
    keys,
    values,
    attn_out,
    out_grad,
    lse,
    trace_id,
    key_tiles,
    tile_count,
    w_query,
    w_key,
    w_value,
    w_out,
):
    tokens_here, width = queries.shape
    heads_here = width // HD
    seq_count = lax.axis_size("seq")
    seq_index = lax.axis_index("seq")
    tiles_here = tokens_here // TILE
    head_count = lax.axis_size("head")
    head_index = lax.axis_index("head")
    grad_blocks = [out_grad] + [from_behind(out_grad, "head", shift) for shift in range(1, head_count)]
    block_order = (head_index - jnp.arange(head_count)) % head_count
    block_width = out_grad.shape[1]
    w_out_blocks = jnp.take(
        w_out.reshape(w_out.shape[0], head_count, block_width), block_order, axis=1
    ).reshape(w_out.shape[0], head_count * block_width)
    d_attn = lax.dot_general(
        jnp.concatenate(grad_blocks, axis=1),
        w_out_blocks,
        (((1,), (1,)), ((), ())),
        preferred_element_type=jnp.float32,
    ).astype(jnp.bfloat16)
    product = d_attn.astype(jnp.float32) * attn_out.astype(jnp.float32)
    delta = jnp.sum(product.reshape(tokens_here, heads_here, HD), axis=2).T
    query_heads = queries.reshape(tokens_here, heads_here, HD)
    key_heads = keys.reshape(tokens_here, heads_here, HD)
    value_heads = values.reshape(tokens_here, heads_here, HD)
    grad_heads = d_attn.reshape(tokens_here, heads_here, HD)
    trace_here = lax.dynamic_slice_in_dim(trace_id, seq_index * tokens_here, tokens_here, 0)
    slots = jnp.arange(SEL)[None, :] < tile_count[:, None]
    tile_range = jnp.arange(seq_count * tiles_here)
    allowed = jnp.any(
        (key_tiles[:, :, None] == tile_range[None, None, :]) & slots[:, :, None], axis=1
    )

    kv_all = lax.all_gather(jnp.stack([key_heads, value_heads]), "seq", axis=1, tiled=True)
    qg_all = lax.all_gather(jnp.stack([query_heads, grad_heads]), "seq", axis=1, tiled=True)
    grad_all = qg_all[1]
    stats = jnp.concatenate(
        [lse, delta, allowed.astype(jnp.float32).reshape(-1, tokens_here)], axis=0
    )
    stats_all = lax.all_gather(stats, "seq", axis=1, tiled=True)
    total_tokens = kv_all.shape[1]
    lse_all = stats_all[:heads_here]
    delta_all = stats_all[heads_here:2 * heads_here]
    allowed_all = stats_all[2 * heads_here:].reshape(seq_count, tiles_here, -1)
    allowed_all = allowed_all.reshape(seq_count * tiles_here, -1)[:, : seq_count * tiles_here] > 0.5
    chunk = min(total_tokens, 8192)
    query_sum = None
    for first in range(0, total_tokens, chunk):
        listed = allowed[:, first // TILE:(first + chunk) // TILE]
        admit = jnp.repeat(jnp.repeat(listed, TILE, axis=0), TILE, axis=1) & (
            trace_here[:, None] != trace_id[None, first:first + chunk]
        )
        query_add = query_grads(
            query_heads, kv_all[0, first:first + chunk], kv_all[1, first:first + chunk],
            grad_heads, lse, delta, admit,
        )
        query_sum = query_add if query_sum is None else query_sum + query_add
    key_sum = None
    mine = seq_index * tiles_here
    chunk = min(total_tokens, 8192)
    for first in range(0, total_tokens, chunk):
        listed = lax.dynamic_slice_in_dim(allowed_all[first // TILE:(first + chunk) // TILE], mine, tiles_here, 1)
        admit = jnp.repeat(jnp.repeat(listed.T, TILE, axis=0), TILE, axis=1) & (
            trace_here[:, None] != trace_id[None, first:first + chunk]
        )
        key_add, value_add = key_grads(
            qg_all[0, first:first + chunk], key_heads, value_heads, grad_all[first:first + chunk],
            lse_all[:, first:first + chunk], delta_all[:, first:first + chunk], admit,
        )
        if key_sum is None:
            key_sum, value_sum = key_add, value_add
        else:
            key_sum, value_sum = key_sum + key_add, value_sum + value_add
    d_query = query_sum.astype(jnp.bfloat16).reshape(tokens_here, width)
    d_key = key_sum.astype(jnp.bfloat16).reshape(tokens_here, width)
    d_value = value_sum.astype(jnp.bfloat16).reshape(tokens_here, width)
    contract = (((1,), (1,)), ((), ()))
    total = lax.dot_general(w_query, d_query, contract, preferred_element_type=jnp.float32)
    total = total + lax.dot_general(w_key, d_key, contract, preferred_element_type=jnp.float32)
    total = total + lax.dot_general(w_value, d_value, contract, preferred_element_type=jnp.float32)
    total = total.reshape((head_count, total.shape[0] // head_count) + total.shape[1:])
    total = total.astype(jnp.bfloat16)
    d_input = lax.dynamic_index_in_dim(total, head_index, 0, keepdims=False).astype(jnp.float32)
    for shift in range(1, head_count):
        owed = lax.dynamic_index_in_dim(total, (head_index + shift) % head_count, 0, keepdims=False)
        d_input = d_input + from_behind(owed, "head", shift).astype(jnp.float32)
    return d_input.T.astype(jnp.bfloat16)


def solution(mesh):
    in_specs = (
        P("seq", "head"),
        P("seq", "head"),
        P("seq", "head"),
        P("seq", "head"),
        P("seq", "head"),
        P("head", "seq"),
        P(),
        P("seq", None),
        P("seq"),
        P(None, "head"),
        P(None, "head"),
        P(None, "head"),
        P("head", None),
    )
    out_specs = P("seq", "head")
    return jax.shard_map(
        per_device, mesh=mesh, in_specs=in_specs, out_specs=out_specs, check_vma=False
    )
```
